32 devices in a mesh: grp: 2 (over y), seq: 4 (over z), head: 4 (over x, core).
Axes of the slice: x: 2, y: 2, z: 4, core: 2. Of those that a mesh axis runs over, the one named last changes fastest.
Arguments:
- lin_query: bfloat16 [2560, 8192], P(('grp', 'seq'), 'head'), parts along dimension 0, may hold values from -6 to 6
- lin_key: bfloat16 [2560, 8192], P(('grp', 'seq'), 'head'), parts along dimension 0, may hold values from -6 to 6
- lin_value: bfloat16 [2560, 8192], P(('grp', 'seq'), 'head'), parts along dimension 0, may hold values from -6 to 6
- norm_gain: bfloat16 [8192], P('head'), may hold values from 0.25 to 1.75
- out_gate: bfloat16 [2560, 8192], P(('grp', 'seq'), 'head'), parts along dimension 0, may hold values from -6 to 6
- soft_query: bfloat16 [2560, 8192], P(('grp', 'seq'), 'head'), parts along dimension 0, may hold values from -24 to 24
- soft_key: bfloat16 [2560, 8192], P(('grp', 'seq'), 'head'), parts along dimension 0, may hold values from -24 to 24
- doc_id: int32 [2560], P(('grp', 'seq')), parts along dimension 0, may hold values from 0 to 7, never falling along the last dimension, each value on 1 to 640 neighbouring positions
Outputs:
- lin_out: bfloat16 [2560, 8192], P(('grp', 'seq'), 'head'), parts along dimension 0
- soft_out: bfloat16 [2560, 8192], P(('grp', 'seq'), 'head'), parts along dimension 0
The draws below stay inside these ranges and needn't reach their ends.
There are 2 independent parts, one for each index of `grp`. The reference program is written for one: setup_inputs(seed, part) draws one part's arguments, and reference() takes and returns one part's arrays. A program takes and returns all parts, laid end to end along the dimension named above; an argument that names none is the same for every part. Nothing has to cross between parts.
Inputs may be any that keep to these rules, and one draw needn't show every extreme that they name: `doc_id`: never falls along the sequence; every document holds 1 to half of 1280 tokens, and one holds exactly half of 1280.
All inputs are finite; a program needn't handle non-finite values.
Results may differ from the reference program's by a relative error of at most 0.0095.
Values may be sent and summed in bfloat16 or wider, within the bound.
No kernel may reach another device: no remote copies, remote signals or barrier semaphores. Data moves between devices by JAX's collectives and lax.ppermute only.
A program may use at most 192 MiB of HBM per device.

```python
import math
import jax
import jax.numpy as jnp
import numpy as np
from jax import lax

HEADS = 64
HD = 128
TOK_DEV = 320
LENGTH = 1280
N_SEQ = 4


def drawn_pair(key):
    shape = (LENGTH, HEADS * HD)
    query_rows = jnp.clip(jax.random.normal(jax.random.fold_in(key, 11), shape, jnp.float32), -6.0, 6.0)
    key_rows = jnp.clip(jax.random.normal(jax.random.fold_in(key, 12), shape, jnp.float32), -6.0, 6.0)
    return (query_rows, key_rows)


def draw_soft_query(key, part):
    return drawn_pair(key)[0].astype(jnp.bfloat16)


def draw_soft_key(key, part):
    return drawn_pair(key)[1].astype(jnp.bfloat16)


def level_of(own_key, extent, cuts, smallest, top_value):
    level = 1.0
    for axis_at, parts in cuts:
        heights = jax.random.uniform(jax.random.fold_in(jax.random.fold_in(own_key, 6), axis_at), (parts,), jnp.float32, smallest / len(cuts), top_value / len(cuts))
        level = level * jnp.repeat(jnp.exp(heights), extent[axis_at] // parts).reshape((-1,) + (1,) * (len(extent) - 1 - axis_at))
    return level


def length_profile(count, total, bound, lean):
    portions = [(1 << 20) // math.isqrt(grade ** lean) + 1 for grade in range(2, count + 1)]
    spare, holding = total - bound - (count - 1), [1] * (count - 1)
    while spare > 0:
        movable = [i for i in range(count - 1) if holding[i] < bound]
        whole, remaining = sum([portions[i] for i in movable]), spare
        for i in movable:
            more = min(bound - holding[i], max(1, remaining * portions[i] // whole), spare)
            holding[i] = holding[i] + more
            spare = spare - more
    return np.array([bound] + holding)


def uneven_parts(own_key, amount, total, limit, lean):
    if amount == 2:
        one = jax.random.randint(own_key, (), max(1, total - limit), min(limit, total - 1) + 1)
        return jnp.stack([one, total - one])
    lengths = jnp.asarray(length_profile(amount, total, limit, lean), jnp.int32)
    twos = (amount - 1) // 2
    source_of, sink = lengths[1:1 + 2 * twos:2], lengths[2:2 + 2 * twos:2]
    margin = jnp.minimum(source_of - 1, limit - sink)
    moved = jax.random.randint(jax.random.fold_in(own_key, 1), (twos,), 0, 1 << 20) % (margin + 1)
    lengths = lengths.at[1:1 + 2 * twos:2].set(source_of - moved).at[2:2 + 2 * twos:2].set(sink + moved)
    return lengths[jax.random.permutation(jax.random.fold_in(own_key, 2), amount)]


def normal_values(rng, dims, scale, reach, cuts=(), kind=jnp.bfloat16):
    entries = scale * jax.random.normal(rng, dims, jnp.float32)
    if cuts:
        entries = entries * level_of(rng, dims, cuts, -0.22, 0.18)
    return jnp.clip(entries, -reach, reach).astype(kind)


def setup_inputs(seed: int = 0, part: int = 0) -> dict:
    arg_keys = jax.random.split(jax.random.key(seed), 9)
    own_keys = jax.random.split(jax.random.fold_in(arg_keys[8], part), 9)
    lin_query = normal_values(own_keys[0], (LENGTH, HEADS * HD), 1.0, 6.0, ((0, 4), (1, 4)))
    lin_key = normal_values(own_keys[1], (LENGTH, HEADS * HD), 1.0, 6.0, ((0, 4), (1, 4)))
    lin_value = normal_values(own_keys[2], (LENGTH, HEADS * HD), 1.0, 6.0, ((0, 4), (1, 4)))
    norm_gain = jnp.clip(1.0 + 0.15 * jax.random.normal(arg_keys[3], (HEADS * HD,), jnp.float32), 0.25, 1.75).astype(jnp.bfloat16)
    out_gate = normal_values(own_keys[4], (LENGTH, HEADS * HD), 1.5, 6.0, ((0, 4), (1, 4)))
    soft_query = draw_soft_query(jax.random.fold_in(jax.random.fold_in(arg_keys[8], part), 71), part)
    soft_key = draw_soft_key(jax.random.fold_in(jax.random.fold_in(arg_keys[8], part), 71), part)
    doc_id = jnp.searchsorted(jnp.cumsum(uneven_parts(own_keys[7], 2 * N_SEQ, LENGTH, LENGTH // 2, 1)), jnp.arange(LENGTH), side="right").astype(jnp.int32)
    return {"lin_query": lin_query, "lin_key": lin_key, "lin_value": lin_value, "norm_gain": norm_gain, "out_gate": out_gate, "soft_query": soft_query, "soft_key": soft_key, "doc_id": doc_id}


norm_eps = 1e-06

def lightning_layer(lin_query, lin_key, lin_value, norm_gain, out_gate, doc_id):
    blocks = LENGTH // TOK_DEV

    def split(array):
        return array.reshape(blocks, TOK_DEV, HEADS, HD)
    positions = jnp.arange(TOK_DEV, dtype=jnp.int32)
    causal = positions[:, None] >= positions[None, :]
    doc_blocks = doc_id.reshape(blocks, TOK_DEV)

    def advance(running, block):
        run_state, run_tag = running
        queries, key_rows, value_rows, docs = block
        first_doc = docs[0]
        last_doc = docs[-1]
        carried = jnp.where(first_doc == run_tag, run_state, jnp.zeros_like(run_state))
        scores = jnp.einsum('qhd,khd->hqk', queries.astype(jnp.float32), key_rows.astype(jnp.float32))
        keep_mask = causal & (docs[:, None] == docs[None, :])
        rounded = jnp.where(keep_mask[None], scores, jnp.zeros_like(scores)).astype(jnp.bfloat16)
        rounded = lax.optimization_barrier(rounded)
        block_term = jnp.einsum('hqk,khd->qhd', rounded.astype(jnp.float32), value_rows.astype(jnp.float32))
        carried_term = jnp.einsum('qhd,hde->qhe', queries.astype(jnp.float32), carried, precision=lax.Precision.HIGHEST)
        carried_term = jnp.where((docs == first_doc)[:, None, None], carried_term, jnp.zeros_like(carried_term))
        key_float = key_rows.astype(jnp.float32)
        tail_keys = jnp.where((docs == last_doc)[:, None, None], key_float, jnp.zeros_like(key_float))
        local_state = jnp.einsum('thd,the->hde', tail_keys, value_rows.astype(jnp.float32))
        new_state = local_state + jnp.where(last_doc == run_tag, run_state, jnp.zeros_like(run_state))
        return ((new_state, last_doc), block_term + carried_term)
    start_state = (jnp.zeros((HEADS, HD, HD), jnp.float32), jnp.array(-1, jnp.int32))
    ignored, raw_blocks = lax.scan(advance, start_state, (split(lin_query), split(lin_key), split(lin_value), doc_blocks))
    lin_raw = raw_blocks.reshape(LENGTH, HEADS, HD)
    mean_square = lax.optimization_barrier(jnp.mean(lin_raw * lin_raw, axis=-1, keepdims=True))
    gain_rows = norm_gain.astype(jnp.float32).reshape(HEADS, HD)
    gate_rows = jax.nn.sigmoid(out_gate.astype(jnp.float32).reshape(LENGTH, HEADS, HD))
    normed = lin_raw * lax.rsqrt(mean_square + norm_eps) * gain_rows * gate_rows
    return normed.astype(jnp.bfloat16).reshape(LENGTH, HEADS * HD)

def softmax_layer(soft_query, soft_key, lin_out, doc_id):
    blocks = LENGTH // TOK_DEV
    key_all = soft_key.reshape(LENGTH, HEADS, HD).astype(jnp.float32)
    value_all = lin_out.reshape(LENGTH, HEADS, HD).astype(jnp.float32)
    key_pos = jnp.arange(LENGTH, dtype=jnp.int32)
    score_scale = 1.0 / math.sqrt(HD)

    def one_block(index):
        begin = (index * TOK_DEV).astype(jnp.int32)
        queries = lax.dynamic_slice_in_dim(soft_query, begin, TOK_DEV, 0).reshape(TOK_DEV, HEADS, HD).astype(jnp.float32)
        query_docs = lax.dynamic_slice_in_dim(doc_id, begin, TOK_DEV, 0)
        query_pos = begin + jnp.arange(TOK_DEV, dtype=jnp.int32)
        logits = jnp.einsum('qhd,khd->hqk', queries, key_all) * score_scale
        keep_mask = (query_pos[:, None] >= key_pos[None, :]) & (query_docs[:, None] == doc_id[None, :])
        logits = jnp.where(keep_mask[None], logits, -1e+30)
        row_max = lax.optimization_barrier(jnp.max(logits, axis=-1, keepdims=True))
        expo = jnp.where(keep_mask[None], jnp.exp(logits - row_max), 0.0)
        denom = lax.optimization_barrier(jnp.sum(expo, axis=-1))
        rounded = lax.optimization_barrier(expo.astype(jnp.bfloat16))
        mixed = jnp.einsum('hqk,khd->qhd', rounded.astype(jnp.float32), value_all)
        result = mixed / jnp.transpose(denom)[:, :, None]
        return result.astype(jnp.bfloat16).reshape(TOK_DEV, HEADS * HD)
    outputs = lax.map(one_block, jnp.arange(blocks, dtype=jnp.int32))
    return outputs.reshape(LENGTH, HEADS * HD)

def reference(lin_query, lin_key, lin_value, norm_gain, out_gate, soft_query, soft_key, doc_id):
    lin_out = lightning_layer(lin_query, lin_key, lin_value, norm_gain, out_gate, doc_id)
    soft_out = softmax_layer(soft_query, soft_key, lin_out, doc_id)
    return (lin_out, soft_out)
```

```python
import math

import jax
import jax.numpy as jnp
from jax import lax
from jax.sharding import PartitionSpec as P

HD = 128


norm_eps = 1e-06


def shift_from_below(x, dist, n_seq):
    return lax.ppermute(x, "seq", [(s, s + dist) for s in range(n_seq - dist)])


def per_device(lin_query, lin_key, lin_value, norm_gain, out_gate, soft_query, soft_key, doc_id):
    row_count = lin_query.shape[0]
    head_count = lin_query.shape[1] // HD
    n_seq = lax.axis_size("seq")
    my_index = lax.axis_index("seq")
    max_doc = n_seq * row_count // 2
    reach = min(n_seq - 1, (max_doc + row_count - 2) // row_count)
    dists = list(range(1, reach + 1))

    queries = lin_query.reshape(row_count, head_count, HD)
    key_rows = lin_key.reshape(row_count, head_count, HD)
    value_rows = lin_value.reshape(row_count, head_count, HD)
    first_doc = doc_id[0]
    last_doc = doc_id[-1]

    soft_key_rows = soft_key.reshape(row_count, head_count, HD)
    key_blocks = [soft_key_rows] + [shift_from_below(soft_key_rows, d, n_seq) for d in dists]
    doc_blocks = [doc_id] + [shift_from_below(doc_id, d, n_seq) for d in dists]

    tail_keys = jnp.where((doc_id == last_doc)[:, None, None], key_rows, jnp.zeros_like(key_rows))
    local_state = jnp.einsum(
        "thd,the->hde", tail_keys, value_rows, preferred_element_type=jnp.float32
    )
    state_bf = local_state.astype(jnp.bfloat16)
    carried = jnp.zeros_like(local_state)
    for d in dists:
        state_in = shift_from_below(state_bf, d, n_seq).astype(jnp.float32)
        wanted = (my_index >= d) & (doc_blocks[d][-1] == first_doc)
        carried = carried + jnp.where(wanted, state_in, jnp.zeros_like(state_in))

    positions = jnp.arange(row_count, dtype=jnp.int32)
    causal = positions[:, None] >= positions[None, :]
    keep_local = causal & (doc_id[:, None] == doc_id[None, :])
    scores = jnp.einsum("qhd,khd->hqk", queries, key_rows, preferred_element_type=jnp.float32)
    rounded = jnp.where(keep_local[None], scores, jnp.zeros_like(scores)).astype(jnp.bfloat16)
    block_term = jnp.einsum("hqk,khd->qhd", rounded, value_rows, preferred_element_type=jnp.float32)
    carried_term = jnp.einsum(
        "qhd,hde->qhe", queries.astype(jnp.float32), carried, precision=lax.Precision.HIGHEST
    )
    carried_term = jnp.where(
        (doc_id == first_doc)[:, None, None], carried_term, jnp.zeros_like(carried_term)
    )
    lin_raw = block_term + carried_term
    mean_square = jnp.mean(lin_raw * lin_raw, axis=-1, keepdims=True)
    gain_rows = norm_gain.astype(jnp.float32).reshape(head_count, HD)
    gate_rows = jax.nn.sigmoid(out_gate.astype(jnp.float32).reshape(row_count, head_count, HD))
    normed = lin_raw * lax.rsqrt(mean_square + norm_eps) * gain_rows * gate_rows
    lin_out = normed.astype(jnp.bfloat16).reshape(row_count, head_count * HD)

    value_own = lin_out.reshape(row_count, head_count, HD)
    value_blocks = [value_own] + [shift_from_below(value_own, d, n_seq) for d in dists]

    query_soft = soft_query.reshape(row_count, head_count, HD)
    score_scale = 1.0 / math.sqrt(HD)
    key_part = jnp.concatenate(key_blocks, axis=0)
    value_part = jnp.concatenate(value_blocks, axis=0)
    key_docs = jnp.concatenate(doc_blocks, axis=0)
    valid = jnp.concatenate(
        [jnp.full((row_count,), my_index >= d, jnp.bool_) for d in [0] + dists]
    )
    key_off = jnp.concatenate([positions - d * row_count for d in [0] + dists])
    keep_mask = (
        (positions[:, None] >= key_off[None, :])
        & (doc_id[:, None] == key_docs[None, :])
        & valid[None, :]
    )
    logits = (
        jnp.einsum("qhd,khd->hqk", query_soft, key_part, preferred_element_type=jnp.float32)
        * score_scale
    )
    logits = jnp.where(keep_mask[None], logits, -1e30)
    row_max = jnp.max(logits, axis=-1)
    probs = jnp.where(keep_mask[None], jnp.exp(logits - row_max[..., None]), 0.0)
    denom_sum = jnp.sum(probs, axis=-1)
    update = jnp.einsum(
        "hqk,khd->qhd", probs.astype(jnp.bfloat16), value_part, preferred_element_type=jnp.float32
    )
    soft_out = update / jnp.transpose(denom_sum)[:, :, None]
    return (lin_out, soft_out.astype(jnp.bfloat16).reshape(row_count, head_count * HD))


def solution(mesh):
    return jax.shard_map(
        per_device,
        mesh=mesh,
        in_specs=(
            P(("grp", "seq"), "head"),
            P(("grp", "seq"), "head"),
            P(("grp", "seq"), "head"),
            P("head"),
            P(("grp", "seq"), "head"),
            P(("grp", "seq"), "head"),
            P(("grp", "seq"), "head"),
            P(("grp", "seq")),
        ),
        out_specs=(P(("grp", "seq"), "head"), P(("grp", "seq"), "head")),
        check_vma=False,
    )
```

```python
import math

import jax
import jax.numpy as jnp
from jax import lax
from jax.sharding import PartitionSpec as P

HD = 128


norm_eps = 1e-06


def shift_up(x, dist, n_seq):
    return lax.ppermute(x, "seq", [(s, s + dist) for s in range(n_seq - dist)])


def shift_down(x, dist, n_seq):
    return lax.ppermute(x, "seq", [(s + dist, s) for s in range(n_seq - dist)])


def merge(part_a, part_b):
    out_a, max_a, sum_a = part_a
    out_b, max_b, sum_b = part_b
    top = jnp.maximum(max_a, max_b)
    scale_a = jnp.exp(max_a - top)
    scale_b = jnp.exp(max_b - top)
    out = out_a * jnp.transpose(scale_a)[:, :, None] + out_b * jnp.transpose(scale_b)[:, :, None]
    return out, top, sum_a * scale_a + sum_b * scale_b


def per_device(lin_query, lin_key, lin_value, norm_gain, out_gate, soft_query, soft_key, doc_id):
    row_count = lin_query.shape[0]
    head_count = lin_query.shape[1] // HD
    n_seq = lax.axis_size("seq")
    my_index = lax.axis_index("seq")
    max_doc = n_seq * row_count // 2
    reach = min(n_seq - 1, (max_doc + row_count - 2) // row_count)
    dists = list(range(1, reach + 1))

    queries = lin_query.reshape(row_count, head_count, HD)
    key_rows = lin_key.reshape(row_count, head_count, HD)
    value_rows = lin_value.reshape(row_count, head_count, HD)
    first_doc = doc_id[0]
    last_doc = doc_id[-1]

    query_soft = soft_query.reshape(row_count, head_count, HD)
    query_blocks = [query_soft]
    for d in dists:
        query_blocks.append(shift_down(query_blocks[-1], 1, n_seq))
    query_docs = [doc_id] + [shift_down(doc_id, d, n_seq) for d in dists]

    tail_keys = jnp.where((doc_id == last_doc)[:, None, None], key_rows, jnp.zeros_like(key_rows))
    local_state = jnp.einsum(
        "thd,the->hde", tail_keys, value_rows, preferred_element_type=jnp.float32
    )
    state_bf = local_state.astype(jnp.bfloat16)
    carried = jnp.zeros_like(local_state)
    for d in dists:
        state_in = shift_up(state_bf, d, n_seq).astype(jnp.float32)
        tag_in = shift_up(last_doc[None], d, n_seq)[0]
        wanted = (my_index >= d) & (tag_in == first_doc)
        carried = carried + jnp.where(wanted, state_in, jnp.zeros_like(state_in))

    positions = jnp.arange(row_count, dtype=jnp.int32)
    causal = positions[:, None] >= positions[None, :]
    keep_local = causal & (doc_id[:, None] == doc_id[None, :])

    score_scale = 1.0 / math.sqrt(HD)
    key_soft = soft_key.reshape(row_count, head_count, HD)
    weights = []
    for d in [0] + dists:
        keep = query_docs[d][:, None] == doc_id[None, :]
        if d == 0:
            keep = keep & causal
        logits = (
            jnp.einsum(
                "qhd,khd->hqk", query_blocks[d], key_soft, preferred_element_type=jnp.float32
            )
            * score_scale
        )
        logits = jnp.where(keep[None], logits, -1e30)
        row_max = jnp.max(logits, axis=-1)
        probs = jnp.where(keep[None], jnp.exp(logits - row_max[..., None]), 0.0)
        weights.append((probs.astype(jnp.bfloat16), row_max, jnp.sum(probs, axis=-1)))

    scores = jnp.einsum("qhd,khd->hqk", queries, key_rows, preferred_element_type=jnp.float32)
    rounded = jnp.where(keep_local[None], scores, jnp.zeros_like(scores)).astype(jnp.bfloat16)
    block_term = jnp.einsum("hqk,khd->qhd", rounded, value_rows, preferred_element_type=jnp.float32)
    carried_term = jnp.einsum(
        "qhd,hde->qhe", queries.astype(jnp.float32), carried, precision=lax.Precision.HIGHEST
    )
    carried_term = jnp.where(
        (doc_id == first_doc)[:, None, None], carried_term, jnp.zeros_like(carried_term)
    )
    lin_raw = block_term + carried_term
    mean_square = jnp.mean(lin_raw * lin_raw, axis=-1, keepdims=True)
    gain_rows = norm_gain.astype(jnp.float32).reshape(head_count, HD)
    gate_rows = jax.nn.sigmoid(out_gate.astype(jnp.float32).reshape(row_count, head_count, HD))
    normed = lin_raw * lax.rsqrt(mean_square + norm_eps) * gain_rows * gate_rows
    lin_out = normed.astype(jnp.bfloat16).reshape(row_count, head_count * HD)
    value_own = lin_out.reshape(row_count, head_count, HD)

    def partial_out(d):
        probs, row_max, row_sum = weights[d]
        mixed = jnp.einsum(
            "hqk,khd->qhd", probs, value_own, preferred_element_type=jnp.float32
        )
        return mixed, row_max, row_sum

    running = None
    for d in reversed([0] + dists):
        part = partial_out(d)
        if running is not None:
            out_in, max_in, sum_in = running
            has_source = my_index >= 1
            max_in = jnp.where(has_source, max_in, -1e30)
            sum_in = jnp.where(has_source, sum_in, 0.0)
            out_in = jnp.where(has_source, out_in.astype(jnp.float32), 0.0)
            part = merge((out_in, max_in, sum_in), part)
        if d > 0:
            out_d, max_d, sum_d = part
            running = (
                shift_up(out_d.astype(jnp.bfloat16), 1, n_seq),
                shift_up(max_d, 1, n_seq),
                shift_up(sum_d, 1, n_seq),
            )
    mixed, row_max, row_sum = part
    soft_out = mixed / jnp.transpose(row_sum)[:, :, None]
    return (lin_out, soft_out.astype(jnp.bfloat16).reshape(row_count, head_count * HD))


def solution(mesh):
    return jax.shard_map(
        per_device,
        mesh=mesh,
        in_specs=(
            P(("grp", "seq"), "head"),
            P(("grp", "seq"), "head"),
            P(("grp", "seq"), "head"),
            P("head"),
            P(("grp", "seq"), "head"),
            P(("grp", "seq"), "head"),
            P(("grp", "seq"), "head"),
            P(("grp", "seq")),
        ),
        out_specs=(P(("grp", "seq"), "head"), P(("grp", "seq"), "head")),
        check_vma=False,
    )
```

```python
import math

import jax
import jax.numpy as jnp
from jax import lax
from jax.sharding import PartitionSpec as P

HD = 128


norm_eps = 1e-06


def shift_up(x, dist, n_seq):
    return lax.ppermute(x, "seq", [(s, s + dist) for s in range(n_seq - dist)])


def shift_down(x, dist, n_seq):
    return lax.ppermute(x, "seq", [(s + dist, s) for s in range(n_seq - dist)])


def merge(part_a, part_b):
    out_a, max_a, sum_a = part_a
    out_b, max_b, sum_b = part_b
    top = jnp.maximum(max_a, max_b)
    scale_a = jnp.exp(max_a - top)
    scale_b = jnp.exp(max_b - top)
    out = out_a * jnp.transpose(scale_a)[:, :, None] + out_b * jnp.transpose(scale_b)[:, :, None]
    return out, top, sum_a * scale_a + sum_b * scale_b


def per_device(lin_query, lin_key, lin_value, norm_gain, out_gate, soft_query, soft_key, doc_id):
    row_count = lin_query.shape[0]
    head_count = lin_query.shape[1] // HD
    n_seq = lax.axis_size("seq")
    my_index = lax.axis_index("seq")
    max_doc = n_seq * row_count // 2
    reach = min(n_seq - 1, (max_doc + row_count - 2) // row_count)
    dists = list(range(1, reach + 1))

    queries = lin_query.reshape(row_count, head_count, HD)
    key_rows = lin_key.reshape(row_count, head_count, HD)
    value_rows = lin_value.reshape(row_count, head_count, HD)
    first_doc = doc_id[0]
    last_doc = doc_id[-1]

    query_soft = soft_query.reshape(row_count, head_count, HD)
    doc_cols = jnp.broadcast_to(doc_id.astype(jnp.bfloat16)[:, None], (row_count, HD))
    message = jnp.concatenate([soft_query, doc_cols], axis=1)
    query_blocks = [query_soft]
    query_docs = [doc_id]
    for d in dists:
        message = shift_down(message, 1, n_seq)
        query_blocks.append(message[:, : head_count * HD].reshape(row_count, head_count, HD))
        query_docs.append(message[:, head_count * HD].astype(jnp.int32))

    tail_keys = jnp.where((doc_id == last_doc)[:, None, None], key_rows, jnp.zeros_like(key_rows))
    local_state = jnp.einsum(
        "thd,the->hde", tail_keys, value_rows, preferred_element_type=jnp.float32
    )
    state_rows = local_state.astype(jnp.bfloat16).reshape(head_count * HD, HD)
    tag_rows = jnp.full((8, HD), last_doc, jnp.int32).astype(jnp.bfloat16)
    state_msg = jnp.concatenate([state_rows, tag_rows], axis=0)
    carried = jnp.zeros_like(local_state)
    for d in dists:
        msg_in = shift_up(state_msg, d, n_seq)
        state_in = msg_in[: head_count * HD].reshape(head_count, HD, HD).astype(jnp.float32)
        tag_in = msg_in[head_count * HD, 0].astype(jnp.int32)
        wanted = (my_index >= d) & (tag_in == first_doc)
        carried = carried + jnp.where(wanted, state_in, jnp.zeros_like(state_in))

    positions = jnp.arange(row_count, dtype=jnp.int32)
    causal = positions[:, None] >= positions[None, :]
    keep_local = causal & (doc_id[:, None] == doc_id[None, :])

    score_scale = 1.0 / math.sqrt(HD)
    key_soft = soft_key.reshape(row_count, head_count, HD)
    weights = []
    for d in [0] + dists:
        keep = query_docs[d][:, None] == doc_id[None, :]
        if d == 0:
            keep = keep & causal
        logits = (
            jnp.einsum(
                "qhd,khd->hqk", query_blocks[d], key_soft, preferred_element_type=jnp.float32
            )
            * score_scale
        )
        logits = jnp.where(keep[None], logits, -1e30)
        row_max = jnp.max(logits, axis=-1)
        probs = jnp.where(keep[None], jnp.exp(logits - row_max[..., None]), 0.0)
        weights.append((probs.astype(jnp.bfloat16), row_max, jnp.sum(probs, axis=-1)))

    scores = jnp.einsum("qhd,khd->hqk", queries, key_rows, preferred_element_type=jnp.float32)
    rounded = jnp.where(keep_local[None], scores, jnp.zeros_like(scores)).astype(jnp.bfloat16)
    block_term = jnp.einsum("hqk,khd->qhd", rounded, value_rows, preferred_element_type=jnp.float32)
    carried_term = jnp.einsum(
        "qhd,hde->qhe", queries.astype(jnp.float32), carried, precision=lax.Precision.HIGHEST
    )
    carried_term = jnp.where(
        (doc_id == first_doc)[:, None, None], carried_term, jnp.zeros_like(carried_term)
    )
    lin_raw = block_term + carried_term
    mean_square = jnp.mean(lin_raw * lin_raw, axis=-1, keepdims=True)
    gain_rows = norm_gain.astype(jnp.float32).reshape(head_count, HD)
    gate_rows = jax.nn.sigmoid(out_gate.astype(jnp.float32).reshape(row_count, head_count, HD))
    normed = lin_raw * lax.rsqrt(mean_square + norm_eps) * gain_rows * gate_rows
    lin_out = normed.astype(jnp.bfloat16).reshape(row_count, head_count * HD)
    value_own = lin_out.reshape(row_count, head_count, HD)

    def partial_out(d):
        probs, row_max, row_sum = weights[d]
        mixed = jnp.einsum(
            "hqk,khd->qhd", probs, value_own, preferred_element_type=jnp.float32
        )
        return mixed, row_max, row_sum

    running = None
    for d in reversed([0] + dists):
        part = partial_out(d)
        if running is not None:
            out_in, stats_in = running
            has_source = my_index >= 1
            max_in = jnp.where(has_source, stats_in[0], -1e30)
            sum_in = jnp.where(has_source, stats_in[1], 0.0)
            out_in = jnp.where(has_source, out_in.astype(jnp.float32), 0.0)
            part = merge((out_in, max_in, sum_in), part)
        if d > 0:
            out_d, max_d, sum_d = part
            running = (
                shift_up(out_d.astype(jnp.bfloat16), 1, n_seq),
                shift_up(jnp.stack([max_d, sum_d]), 1, n_seq),
            )
    mixed, row_max, row_sum = part
    soft_out = mixed / jnp.transpose(row_sum)[:, :, None]
    return (lin_out, soft_out.astype(jnp.bfloat16).reshape(row_count, head_count * HD))


def solution(mesh):
    return jax.shard_map(
        per_device,
        mesh=mesh,
        in_specs=(
            P(("grp", "seq"), "head"),
            P(("grp", "seq"), "head"),
            P(("grp", "seq"), "head"),
            P("head"),
            P(("grp", "seq"), "head"),
            P(("grp", "seq"), "head"),
            P(("grp", "seq"), "head"),
            P(("grp", "seq")),
        ),
        out_specs=(P(("grp", "seq"), "head"), P(("grp", "seq"), "head")),
        check_vma=False,
    )
```

```python
import math

import jax
import jax.numpy as jnp
from jax import lax
from jax.sharding import PartitionSpec as P

HD = 128


norm_eps = 1e-06


def shift_up(x, dist, n_seq):
    return lax.ppermute(x, "seq", [(s, s + dist) for s in range(n_seq - dist)])


def shift_down(x, dist, n_seq):
    return lax.ppermute(x, "seq", [(s + dist, s) for s in range(n_seq - dist)])


def merge(part_a, part_b):
    out_a, max_a, sum_a = part_a
    out_b, max_b, sum_b = part_b
    top = jnp.maximum(max_a, max_b)
    scale_a = jnp.exp(max_a - top)
    scale_b = jnp.exp(max_b - top)
    out = out_a * jnp.transpose(scale_a)[:, :, None] + out_b * jnp.transpose(scale_b)[:, :, None]
    return out, top, sum_a * scale_a + sum_b * scale_b


def per_device(lin_query, lin_key, lin_value, norm_gain, out_gate, soft_query, soft_key, doc_id):
    row_count = lin_query.shape[0]
    head_count = lin_query.shape[1] // HD
    n_seq = lax.axis_size("seq")
    my_index = lax.axis_index("seq")
    max_doc = n_seq * row_count // 2
    reach = min(n_seq - 1, (max_doc + row_count - 2) // row_count)
    dists = list(range(1, reach + 1))

    queries = lin_query.reshape(row_count, head_count, HD)
    key_rows = lin_key.reshape(row_count, head_count, HD)
    value_rows = lin_value.reshape(row_count, head_count, HD)
    first_doc = doc_id[0]
    last_doc = doc_id[-1]

    query_soft = soft_query.reshape(row_count, head_count, HD)
    doc_cols = jnp.broadcast_to(doc_id.astype(jnp.bfloat16)[:, None], (row_count, HD))
    message = jnp.concatenate([soft_query, doc_cols], axis=1)
    query_blocks = [query_soft]
    query_docs = [doc_id]
    for d in dists:
        message = shift_down(message, 1, n_seq)
        query_blocks.append(message[:, : head_count * HD].reshape(row_count, head_count, HD))
        query_docs.append(message[:, head_count * HD].astype(jnp.int32))

    tail_keys = jnp.where((doc_id == last_doc)[:, None, None], key_rows, jnp.zeros_like(key_rows))
    local_state = jnp.einsum(
        "thd,the->hde", tail_keys, value_rows, preferred_element_type=jnp.float32
    )
    state_rows = local_state.astype(jnp.bfloat16).reshape(head_count * HD, HD)
    tag_rows = jnp.full((8, HD), last_doc, jnp.int32).astype(jnp.bfloat16)
    state_msg = jnp.concatenate([state_rows, tag_rows], axis=0)
    carried = jnp.zeros_like(local_state)
    for d in dists:
        msg_in = shift_up(state_msg, d, n_seq)
        state_in = msg_in[: head_count * HD].reshape(head_count, HD, HD).astype(jnp.float32)
        tag_in = msg_in[head_count * HD, 0].astype(jnp.int32)
        wanted = (my_index >= d) & (tag_in == first_doc)
        carried = carried + jnp.where(wanted, state_in, jnp.zeros_like(state_in))

    positions = jnp.arange(row_count, dtype=jnp.int32)
    causal = positions[:, None] >= positions[None, :]
    keep_local = causal & (doc_id[:, None] == doc_id[None, :])

    scores = jnp.einsum("qhd,khd->hqk", queries, key_rows, preferred_element_type=jnp.float32)
    rounded = jnp.where(keep_local[None], scores, jnp.zeros_like(scores)).astype(jnp.bfloat16)
    block_term = jnp.einsum("hqk,khd->qhd", rounded, value_rows, preferred_element_type=jnp.float32)
    block_term = lax.optimization_barrier(block_term)
    carried_term = jnp.einsum(
        "qhd,hde->qhe", queries.astype(jnp.float32), carried, precision=lax.Precision.HIGHEST
    )
    carried_term = jnp.where(
        (doc_id == first_doc)[:, None, None], carried_term, jnp.zeros_like(carried_term)
    )
    lin_raw = block_term + carried_term
    mean_square = jnp.mean(lin_raw * lin_raw, axis=-1, keepdims=True)
    gain_rows = norm_gain.astype(jnp.float32).reshape(head_count, HD)
    gate_rows = jax.nn.sigmoid(out_gate.astype(jnp.float32).reshape(row_count, head_count, HD))
    normed = lin_raw * lax.rsqrt(mean_square + norm_eps) * gain_rows * gate_rows
    lin_out = normed.astype(jnp.bfloat16).reshape(row_count, head_count * HD)
    if len(query_blocks) > 2:
        tied = lax.optimization_barrier((lin_out, query_blocks[2:], query_docs[2:]))
        lin_out = tied[0]
        query_blocks = query_blocks[:2] + list(tied[1])
        query_docs = query_docs[:2] + list(tied[2])
    value_own = lin_out.reshape(row_count, head_count, HD)
    score_scale = 1.0 / math.sqrt(HD)
    key_soft = soft_key.reshape(row_count, head_count, HD)
    weights = []
    for d in [0] + dists:
        keep = query_docs[d][:, None] == doc_id[None, :]
        if d == 0:
            keep = keep & causal
        logits = (
            jnp.einsum(
                "qhd,khd->hqk", query_blocks[d], key_soft, preferred_element_type=jnp.float32
            )
            * score_scale
        )
        logits = jnp.where(keep[None], logits, -1e30)
        row_max = jnp.max(logits, axis=-1)
        probs = jnp.where(keep[None], jnp.exp(logits - row_max[..., None]), 0.0)
        weights.append((probs.astype(jnp.bfloat16), row_max, jnp.sum(probs, axis=-1)))

    def partial_out(d):
        probs, row_max, row_sum = weights[d]
        mixed = jnp.einsum(
            "hqk,khd->qhd", probs, value_own, preferred_element_type=jnp.float32
        )
        return mixed, row_max, row_sum

    running = None
    for d in reversed([0] + dists):
        part = partial_out(d)
        if running is not None:
            out_in, stats_in = running
            has_source = my_index >= 1
            max_in = jnp.where(has_source, stats_in[0], -1e30)
            sum_in = jnp.where(has_source, stats_in[1], 0.0)
            out_in = jnp.where(has_source, out_in.astype(jnp.float32), 0.0)
            part = merge((out_in, max_in, sum_in), part)
        if d > 0:
            out_d, max_d, sum_d = part
            running = (
                shift_up(out_d.astype(jnp.bfloat16), 1, n_seq),
                shift_up(jnp.stack([max_d, sum_d]), 1, n_seq),
            )
    mixed, row_max, row_sum = part
    soft_out = mixed / jnp.transpose(row_sum)[:, :, None]
    return (lin_out, soft_out.astype(jnp.bfloat16).reshape(row_count, head_count * HD))


def solution(mesh):
    return jax.shard_map(
        per_device,
        mesh=mesh,
        in_specs=(
            P(("grp", "seq"), "head"),
            P(("grp", "seq"), "head"),
            P(("grp", "seq"), "head"),
            P("head"),
            P(("grp", "seq"), "head"),
            P(("grp", "seq"), "head"),
            P(("grp", "seq"), "head"),
            P(("grp", "seq")),
        ),
        out_specs=(P(("grp", "seq"), "head"), P(("grp", "seq"), "head")),
        check_vma=False,
    )
```

```python
import math

import jax
import jax.numpy as jnp
from jax import lax
from jax.sharding import PartitionSpec as P

HD = 128


norm_eps = 1e-06


def shift_up(x, dist, n_seq):
    return lax.ppermute(x, "seq", [(s, s + dist) for s in range(n_seq - dist)])


def shift_down(x, dist, n_seq):
    return lax.ppermute(x, "seq", [(s + dist, s) for s in range(n_seq - dist)])


def merge(part_a, part_b):
    out_a, max_a, sum_a = part_a
    out_b, max_b, sum_b = part_b
    top = jnp.maximum(max_a, max_b)
    scale_a = jnp.exp(max_a - top)
    scale_b = jnp.exp(max_b - top)
    out = out_a * jnp.transpose(scale_a)[:, :, None] + out_b * jnp.transpose(scale_b)[:, :, None]
    return out, top, sum_a * scale_a + sum_b * scale_b


def per_device(lin_query, lin_key, lin_value, norm_gain, out_gate, soft_query, soft_key, doc_id):
    row_count = lin_query.shape[0]
    head_count = lin_query.shape[1] // HD
    n_seq = lax.axis_size("seq")
    my_index = lax.axis_index("seq")
    max_doc = n_seq * row_count // 2
    reach = min(n_seq - 1, (max_doc + row_count - 2) // row_count)
    dists = list(range(1, reach + 1))
    width = head_count * HD

    queries = lin_query.reshape(row_count, head_count, HD)
    key_rows = lin_key.reshape(row_count, head_count, HD)
    value_rows = lin_value.reshape(row_count, head_count, HD)
    first_doc = doc_id[0]
    last_doc = doc_id[-1]

    doc_cols = jnp.broadcast_to(doc_id.astype(jnp.bfloat16)[:, None], (row_count, HD))

    tail_keys = jnp.where((doc_id == last_doc)[:, None, None], key_rows, jnp.zeros_like(key_rows))
    local_state = jnp.einsum(
        "thd,the->hde", tail_keys, value_rows, preferred_element_type=jnp.float32
    )
    state_rows = local_state.astype(jnp.bfloat16).reshape(width, HD)
    tag_rows = jnp.full((8, HD), last_doc, jnp.int32).astype(jnp.bfloat16)
    state_msg = jnp.concatenate([state_rows, tag_rows], axis=0)
    carried = jnp.zeros_like(local_state)
    for d in dists:
        msg_in = shift_up(state_msg, d, n_seq)
        state_in = msg_in[:width].reshape(head_count, HD, HD).astype(jnp.float32)
        tag_in = msg_in[width, 0].astype(jnp.int32)
        wanted = (my_index >= d) & (tag_in == first_doc)
        carried = carried + jnp.where(wanted, state_in, jnp.zeros_like(state_in))

    next_msg = shift_down(jnp.concatenate([soft_query, doc_cols], axis=1), 1, n_seq)
    next_queries = next_msg[:, :width].reshape(row_count, head_count, HD)
    next_docs = next_msg[:, width].astype(jnp.int32)
    key_msgs = [jnp.concatenate([soft_key, doc_cols], axis=1)]
    for d in dists[:-1]:
        key_msgs.append(shift_up(key_msgs[-1], 1, n_seq))
    key_blocks = [m[:, :width].reshape(row_count, head_count, HD) for m in key_msgs]
    key_docs = [m[:, width].astype(jnp.int32) for m in key_msgs]

    positions = jnp.arange(row_count, dtype=jnp.int32)
    causal = positions[:, None] >= positions[None, :]
    keep_local = causal & (doc_id[:, None] == doc_id[None, :])
    score_scale = 1.0 / math.sqrt(HD)

    def weights_of(query_rows, keep):
        logits = (
            jnp.einsum("qhd,khd->hqk", query_rows, key_all, preferred_element_type=jnp.float32)
            * score_scale
        )
        logits = jnp.where(keep[None], logits, -1e30)
        row_max = jnp.max(logits, axis=-1)
        probs = jnp.where(keep[None], jnp.exp(logits - row_max[..., None]), 0.0)
        return probs.astype(jnp.bfloat16), row_max, jnp.sum(probs, axis=-1)

    key_all = key_blocks[0]
    diag = weights_of(soft_query.reshape(row_count, head_count, HD), keep_local)
    key_all = jnp.concatenate(key_blocks, axis=0)
    valid = jnp.concatenate(
        [jnp.full((row_count,), my_index >= d, jnp.bool_) for d in range(len(key_blocks))]
    )
    keep_next = (next_docs[:, None] == jnp.concatenate(key_docs)[None, :]) & valid[None, :]
    ahead = weights_of(next_queries, keep_next)

    scores = jnp.einsum("qhd,khd->hqk", queries, key_rows, preferred_element_type=jnp.float32)
    rounded = jnp.where(keep_local[None], scores, jnp.zeros_like(scores)).astype(jnp.bfloat16)
    block_term = jnp.einsum("hqk,khd->qhd", rounded, value_rows, preferred_element_type=jnp.float32)
    carried_term = jnp.einsum(
        "qhd,hde->qhe", queries.astype(jnp.float32), carried, precision=lax.Precision.HIGHEST
    )
    carried_term = jnp.where(
        (doc_id == first_doc)[:, None, None], carried_term, jnp.zeros_like(carried_term)
    )
    lin_raw = block_term + carried_term
    mean_square = jnp.mean(lin_raw * lin_raw, axis=-1, keepdims=True)
    gain_rows = norm_gain.astype(jnp.float32).reshape(head_count, HD)
    gate_rows = jax.nn.sigmoid(out_gate.astype(jnp.float32).reshape(row_count, head_count, HD))
    normed = lin_raw * lax.rsqrt(mean_square + norm_eps) * gain_rows * gate_rows
    lin_out = normed.astype(jnp.bfloat16).reshape(row_count, width)

    value_blocks = [lin_out.reshape(row_count, head_count, HD)]
    for d in dists[:-1]:
        value_blocks.append(shift_up(value_blocks[-1], 1, n_seq))

    probs, ahead_max, ahead_sum = ahead
    ahead_out = jnp.zeros((row_count, head_count, HD), jnp.float32)
    for d, value_block in enumerate(value_blocks):
        ahead_out = ahead_out + jnp.einsum(
            "hqk,khd->qhd",
            probs[:, :, d * row_count : (d + 1) * row_count],
            value_block,
            preferred_element_type=jnp.float32,
        )
    out_in = shift_up(ahead_out.astype(jnp.bfloat16), 1, n_seq)
    stats_in = shift_up(jnp.stack([ahead_max, ahead_sum]), 1, n_seq)
    has_source = my_index >= 1
    max_in = jnp.where(has_source, stats_in[0], -1e30)
    sum_in = jnp.where(has_source, stats_in[1], 0.0)
    out_in = jnp.where(has_source, out_in.astype(jnp.float32), 0.0)

    diag_probs, diag_max, diag_sum = diag
    diag_out = jnp.einsum(
        "hqk,khd->qhd", diag_probs, value_blocks[0], preferred_element_type=jnp.float32
    )
    mixed, row_max, row_sum = merge((out_in, max_in, sum_in), (diag_out, diag_max, diag_sum))
    soft_out = mixed / jnp.transpose(row_sum)[:, :, None]
    return (lin_out, soft_out.astype(jnp.bfloat16).reshape(row_count, width))


def solution(mesh):
    return jax.shard_map(
        per_device,
        mesh=mesh,
        in_specs=(
            P(("grp", "seq"), "head"),
            P(("grp", "seq"), "head"),
            P(("grp", "seq"), "head"),
            P("head"),
            P(("grp", "seq"), "head"),
            P(("grp", "seq"), "head"),
            P(("grp", "seq"), "head"),
            P(("grp", "seq")),
        ),
        out_specs=(P(("grp", "seq"), "head"), P(("grp", "seq"), "head")),
        check_vma=False,
    )
```

```python
import math

import jax
import jax.numpy as jnp
from jax import lax
from jax.sharding import PartitionSpec as P

HD = 128


norm_eps = 1e-06


def shift_up(x, dist, n_seq):
    return lax.ppermute(x, "seq", [(s, s + dist) for s in range(n_seq - dist)])


def shift_down(x, dist, n_seq):
    return lax.ppermute(x, "seq", [(s + dist, s) for s in range(n_seq - dist)])


def merge(part_a, part_b):
    out_a, max_a, sum_a = part_a
    out_b, max_b, sum_b = part_b
    top = jnp.maximum(max_a, max_b)
    scale_a = jnp.exp(max_a - top)
    scale_b = jnp.exp(max_b - top)
    out = out_a * jnp.transpose(scale_a)[:, :, None] + out_b * jnp.transpose(scale_b)[:, :, None]
    return out, top, sum_a * scale_a + sum_b * scale_b


def per_device(lin_query, lin_key, lin_value, norm_gain, out_gate, soft_query, soft_key, doc_id):
    row_count = lin_query.shape[0]
    head_count = lin_query.shape[1] // HD
    n_seq = lax.axis_size("seq")
    my_index = lax.axis_index("seq")
    max_doc = n_seq * row_count // 2
    reach = min(n_seq - 1, (max_doc + row_count - 2) // row_count)
    dists = list(range(1, reach + 1))
    width = head_count * HD

    queries = lin_query.reshape(row_count, head_count, HD)
    key_rows = lin_key.reshape(row_count, head_count, HD)
    value_rows = lin_value.reshape(row_count, head_count, HD)
    first_doc = doc_id[0]
    last_doc = doc_id[-1]

    doc_cols = jnp.broadcast_to(doc_id.astype(jnp.bfloat16)[:, None], (row_count, HD))

    tail_keys = jnp.where((doc_id == last_doc)[:, None, None], key_rows, jnp.zeros_like(key_rows))
    local_state = jnp.einsum(
        "thd,the->hde", tail_keys, value_rows, preferred_element_type=jnp.float32
    )
    tag_rows = jnp.full((8, HD), last_doc, jnp.int32).astype(jnp.bfloat16)
    whole_block = first_doc == last_doc
    running = local_state
    for stage in dists:
        state_rows = running.astype(jnp.bfloat16).reshape(width, HD)
        msg_in = shift_up(jnp.concatenate([state_rows, tag_rows], axis=0), 1, n_seq)
        state_in = msg_in[:width].reshape(head_count, HD, HD).astype(jnp.float32)
        tag_in = msg_in[width, 0].astype(jnp.int32)
        joins = (my_index >= 1) & (tag_in == first_doc)
        if stage < reach:
            running = local_state + jnp.where(joins & whole_block, state_in, 0.0)
        else:
            carried = jnp.where(joins, state_in, jnp.zeros_like(state_in))

    next_msg = shift_down(jnp.concatenate([soft_query, doc_cols], axis=1), 1, n_seq)
    next_queries = next_msg[:, :width].reshape(row_count, head_count, HD)
    next_docs = next_msg[:, width].astype(jnp.int32)
    key_msgs = [jnp.concatenate([soft_key, doc_cols], axis=1)]
    for d in dists[:-1]:
        key_msgs.append(shift_up(key_msgs[-1], 1, n_seq))
    key_blocks = [m[:, :width].reshape(row_count, head_count, HD) for m in key_msgs]
    key_docs = [m[:, width].astype(jnp.int32) for m in key_msgs]

    positions = jnp.arange(row_count, dtype=jnp.int32)
    causal = positions[:, None] >= positions[None, :]
    keep_local = causal & (doc_id[:, None] == doc_id[None, :])
    score_scale = 1.0 / math.sqrt(HD)

    def weights_of(query_rows, keep):
        logits = (
            jnp.einsum("qhd,khd->hqk", query_rows, key_all, preferred_element_type=jnp.float32)
            * score_scale
        )
        logits = jnp.where(keep[None], logits, -1e30)
        row_max = jnp.max(logits, axis=-1)
        probs = jnp.where(keep[None], jnp.exp(logits - row_max[..., None]), 0.0)
        return probs.astype(jnp.bfloat16), row_max, jnp.sum(probs, axis=-1)

    key_all = key_blocks[0]
    diag = weights_of(soft_query.reshape(row_count, head_count, HD), keep_local)
    key_all = jnp.concatenate(key_blocks, axis=0)
    valid = jnp.concatenate(
        [jnp.full((row_count,), my_index >= d, jnp.bool_) for d in range(len(key_blocks))]
    )
    keep_next = (next_docs[:, None] == jnp.concatenate(key_docs)[None, :]) & valid[None, :]
    ahead = weights_of(next_queries, keep_next)

    scores = jnp.einsum("qhd,khd->hqk", queries, key_rows, preferred_element_type=jnp.float32)
    rounded = jnp.where(keep_local[None], scores, jnp.zeros_like(scores)).astype(jnp.bfloat16)
    block_term = jnp.einsum("hqk,khd->qhd", rounded, value_rows, preferred_element_type=jnp.float32)
    carried_term = jnp.einsum(
        "qhd,hde->qhe", queries.astype(jnp.float32), carried, precision=lax.Precision.HIGHEST
    )
    carried_term = jnp.where(
        (doc_id == first_doc)[:, None, None], carried_term, jnp.zeros_like(carried_term)
    )
    lin_raw = block_term + carried_term
    mean_square = jnp.mean(lin_raw * lin_raw, axis=-1, keepdims=True)
    gain_rows = norm_gain.astype(jnp.float32).reshape(head_count, HD)
    gate_rows = jax.nn.sigmoid(out_gate.astype(jnp.float32).reshape(row_count, head_count, HD))
    normed = lin_raw * lax.rsqrt(mean_square + norm_eps) * gain_rows * gate_rows
    lin_out = normed.astype(jnp.bfloat16).reshape(row_count, width)

    value_blocks = [lin_out.reshape(row_count, head_count, HD)]
    for d in dists[:-1]:
        value_blocks.append(shift_up(value_blocks[-1], 1, n_seq))

    probs, ahead_max, ahead_sum = ahead
    ahead_out = jnp.zeros((row_count, head_count, HD), jnp.float32)
    for d, value_block in enumerate(value_blocks):
        ahead_out = ahead_out + jnp.einsum(
            "hqk,khd->qhd",
            probs[:, :, d * row_count : (d + 1) * row_count],
            value_block,
            preferred_element_type=jnp.float32,
        )
    out_in = shift_up(ahead_out.astype(jnp.bfloat16), 1, n_seq)
    stats_in = shift_up(jnp.stack([ahead_max, ahead_sum]), 1, n_seq)
    has_source = my_index >= 1
    max_in = jnp.where(has_source, stats_in[0], -1e30)
    sum_in = jnp.where(has_source, stats_in[1], 0.0)
    out_in = jnp.where(has_source, out_in.astype(jnp.float32), 0.0)

    diag_probs, diag_max, diag_sum = diag
    diag_out = jnp.einsum(
        "hqk,khd->qhd", diag_probs, value_blocks[0], preferred_element_type=jnp.float32
    )
    mixed, row_max, row_sum = merge((out_in, max_in, sum_in), (diag_out, diag_max, diag_sum))
    soft_out = mixed / jnp.transpose(row_sum)[:, :, None]
    return (lin_out, soft_out.astype(jnp.bfloat16).reshape(row_count, width))


def solution(mesh):
    return jax.shard_map(
        per_device,
        mesh=mesh,
        in_specs=(
            P(("grp", "seq"), "head"),
            P(("grp", "seq"), "head"),
            P(("grp", "seq"), "head"),
            P("head"),
            P(("grp", "seq"), "head"),
            P(("grp", "seq"), "head"),
            P(("grp", "seq"), "head"),
            P(("grp", "seq")),
        ),
        out_specs=(P(("grp", "seq"), "head"), P(("grp", "seq"), "head")),
        check_vma=False,
    )
```

```python
import math

import jax
import jax.numpy as jnp
from jax import lax
from jax.sharding import PartitionSpec as P

HD = 128


norm_eps = 1e-06


def shift_up(x, dist, n_seq):
    return lax.ppermute(x, "seq", [(s, s + dist) for s in range(n_seq - dist)])


def shift_down(x, dist, n_seq):
    return lax.ppermute(x, "seq", [(s + dist, s) for s in range(n_seq - dist)])


def merge(part_a, part_b):
    out_a, max_a, sum_a = part_a
    out_b, max_b, sum_b = part_b
    top = jnp.maximum(max_a, max_b)
    scale_a = jnp.exp(max_a - top)
    scale_b = jnp.exp(max_b - top)
    out = out_a * jnp.transpose(scale_a)[:, :, None] + out_b * jnp.transpose(scale_b)[:, :, None]
    return out, top, sum_a * scale_a + sum_b * scale_b


def per_device(lin_query, lin_key, lin_value, norm_gain, out_gate, soft_query, soft_key, doc_id):
    row_count = lin_query.shape[0]
    head_count = lin_query.shape[1] // HD
    n_seq = lax.axis_size("seq")
    my_index = lax.axis_index("seq")
    max_doc = n_seq * row_count // 2
    reach = min(n_seq - 1, (max_doc + row_count - 2) // row_count)
    dists = list(range(1, reach + 1))
    width = head_count * HD

    queries = lin_query.reshape(row_count, head_count, HD)
    key_rows = lin_key.reshape(row_count, head_count, HD)
    value_rows = lin_value.reshape(row_count, head_count, HD)
    first_doc = doc_id[0]
    last_doc = doc_id[-1]

    doc_cols = jnp.broadcast_to(doc_id.astype(jnp.bfloat16)[:, None], (row_count, HD))

    tail_keys = jnp.where((doc_id == last_doc)[:, None, None], key_rows, jnp.zeros_like(key_rows))
    local_state = jnp.einsum(
        "thd,the->hde", tail_keys, value_rows, preferred_element_type=jnp.float32
    )
    tag_rows = jnp.full((8, HD), last_doc, jnp.int32).astype(jnp.bfloat16)
    whole_block = first_doc == last_doc
    running = local_state
    for stage in dists:
        state_rows = running.astype(jnp.bfloat16).reshape(width, HD)
        msg_in = shift_up(jnp.concatenate([state_rows, tag_rows], axis=0), 1, n_seq)
        state_in = msg_in[:width].reshape(head_count, HD, HD).astype(jnp.float32)
        tag_in = msg_in[width, 0].astype(jnp.int32)
        joins = (my_index >= 1) & (tag_in == first_doc)
        if stage < reach:
            running = local_state + jnp.where(joins & whole_block, state_in, 0.0)
        else:
            carried = jnp.where(joins, state_in, jnp.zeros_like(state_in))

    next_msg = shift_down(jnp.concatenate([soft_query, doc_cols], axis=1), 1, n_seq)
    next_queries = next_msg[:, :width].reshape(row_count, head_count, HD)
    next_docs = next_msg[:, width].astype(jnp.int32)
    key_first, _ = lax.optimization_barrier((jnp.concatenate([soft_key, doc_cols], axis=1), carried))
    key_msgs = [key_first]
    for d in dists[:-1]:
        key_msgs.append(shift_up(key_msgs[-1], 1, n_seq))
    key_blocks = [m[:, :width].reshape(row_count, head_count, HD) for m in key_msgs]
    key_docs = [m[:, width].astype(jnp.int32) for m in key_msgs]

    positions = jnp.arange(row_count, dtype=jnp.int32)
    causal = positions[:, None] >= positions[None, :]
    keep_local = causal & (doc_id[:, None] == doc_id[None, :])
    score_scale = 1.0 / math.sqrt(HD)

    def weights_of(query_rows, keep):
        logits = (
            jnp.einsum("qhd,khd->hqk", query_rows, key_all, preferred_element_type=jnp.float32)
            * score_scale
        )
        logits = jnp.where(keep[None], logits, -1e30)
        row_max = jnp.max(logits, axis=-1)
        probs = jnp.where(keep[None], jnp.exp(logits - row_max[..., None]), 0.0)
        return probs.astype(jnp.bfloat16), row_max, jnp.sum(probs, axis=-1)

    key_all = key_blocks[0]
    diag = weights_of(soft_query.reshape(row_count, head_count, HD), keep_local)
    key_all = jnp.concatenate(key_blocks, axis=0)
    valid = jnp.concatenate(
        [jnp.full((row_count,), my_index >= d, jnp.bool_) for d in range(len(key_blocks))]
    )
    keep_next = (next_docs[:, None] == jnp.concatenate(key_docs)[None, :]) & valid[None, :]
    ahead = weights_of(next_queries, keep_next)

    scores = jnp.einsum("qhd,khd->hqk", queries, key_rows, preferred_element_type=jnp.float32)
    rounded = jnp.where(keep_local[None], scores, jnp.zeros_like(scores)).astype(jnp.bfloat16)
    block_term = jnp.einsum("hqk,khd->qhd", rounded, value_rows, preferred_element_type=jnp.float32)
    carried_term = jnp.einsum(
        "qhd,hde->qhe", queries.astype(jnp.float32), carried, precision=lax.Precision.HIGHEST
    )
    carried_term = jnp.where(
        (doc_id == first_doc)[:, None, None], carried_term, jnp.zeros_like(carried_term)
    )
    lin_raw = block_term + carried_term
    mean_square = jnp.mean(lin_raw * lin_raw, axis=-1, keepdims=True)
    gain_rows = norm_gain.astype(jnp.float32).reshape(head_count, HD)
    gate_rows = jax.nn.sigmoid(out_gate.astype(jnp.float32).reshape(row_count, head_count, HD))
    normed = lin_raw * lax.rsqrt(mean_square + norm_eps) * gain_rows * gate_rows
    lin_out = normed.astype(jnp.bfloat16).reshape(row_count, width)

    value_blocks = [lin_out.reshape(row_count, head_count, HD)]
    for d in dists[:-1]:
        value_blocks.append(shift_up(value_blocks[-1], 1, n_seq))

    probs, ahead_max, ahead_sum = ahead
    ahead_out = jnp.zeros((row_count, head_count, HD), jnp.float32)
    for d, value_block in enumerate(value_blocks):
        ahead_out = ahead_out + jnp.einsum(
            "hqk,khd->qhd",
            probs[:, :, d * row_count : (d + 1) * row_count],
            value_block,
            preferred_element_type=jnp.float32,
        )
    out_in = shift_up(ahead_out.astype(jnp.bfloat16), 1, n_seq)
    stats_in = shift_up(jnp.stack([ahead_max, ahead_sum]), 1, n_seq)
    has_source = my_index >= 1
    max_in = jnp.where(has_source, stats_in[0], -1e30)
    sum_in = jnp.where(has_source, stats_in[1], 0.0)
    out_in = jnp.where(has_source, out_in.astype(jnp.float32), 0.0)

    diag_probs, diag_max, diag_sum = diag
    diag_out = jnp.einsum(
        "hqk,khd->qhd", diag_probs, value_blocks[0], preferred_element_type=jnp.float32
    )
    mixed, row_max, row_sum = merge((out_in, max_in, sum_in), (diag_out, diag_max, diag_sum))
    soft_out = mixed / jnp.transpose(row_sum)[:, :, None]
    return (lin_out, soft_out.astype(jnp.bfloat16).reshape(row_count, width))


def solution(mesh):
    return jax.shard_map(
        per_device,
        mesh=mesh,
        in_specs=(
            P(("grp", "seq"), "head"),
            P(("grp", "seq"), "head"),
            P(("grp", "seq"), "head"),
            P("head"),
            P(("grp", "seq"), "head"),
            P(("grp", "seq"), "head"),
            P(("grp", "seq"), "head"),
            P(("grp", "seq")),
        ),
        out_specs=(P(("grp", "seq"), "head"), P(("grp", "seq"), "head")),
        check_vma=False,
    )
```

```python
import math

import jax
import jax.numpy as jnp
from jax import lax
from jax.sharding import PartitionSpec as P

HD = 128


norm_eps = 1e-06


def shift_up(x, dist, n_seq):
    return lax.ppermute(x, "seq", [(s, s + dist) for s in range(n_seq - dist)])


def shift_down(x, dist, n_seq):
    return lax.ppermute(x, "seq", [(s + dist, s) for s in range(n_seq - dist)])


def merge(part_a, part_b):
    out_a, max_a, sum_a = part_a
    out_b, max_b, sum_b = part_b
    top = jnp.maximum(max_a, max_b)
    scale_a = jnp.exp(max_a - top)
    scale_b = jnp.exp(max_b - top)
    out = out_a * jnp.transpose(scale_a)[:, :, None] + out_b * jnp.transpose(scale_b)[:, :, None]
    return out, top, sum_a * scale_a + sum_b * scale_b


def per_device(lin_query, lin_key, lin_value, norm_gain, out_gate, soft_query, soft_key, doc_id):
    row_count = lin_query.shape[0]
    head_count = lin_query.shape[1] // HD
    n_seq = lax.axis_size("seq")
    my_index = lax.axis_index("seq")
    max_doc = n_seq * row_count // 2
    reach = min(n_seq - 1, (max_doc + row_count - 2) // row_count)
    dists = list(range(1, reach + 1))
    width = head_count * HD

    queries = lin_query.reshape(row_count, head_count, HD)
    key_rows = lin_key.reshape(row_count, head_count, HD)
    value_rows = lin_value.reshape(row_count, head_count, HD)
    first_doc = doc_id[0]
    last_doc = doc_id[-1]

    doc_cols = jnp.broadcast_to(doc_id.astype(jnp.bfloat16)[:, None], (row_count, HD))

    tail_keys = jnp.where((doc_id == last_doc)[:, None, None], key_rows, jnp.zeros_like(key_rows))
    local_state = jnp.einsum(
        "thd,the->hde", tail_keys, value_rows, preferred_element_type=jnp.float32
    )
    tag_rows = jnp.full((8, HD), last_doc, jnp.int32).astype(jnp.bfloat16)
    whole_block = first_doc == last_doc
    running = local_state
    for stage in dists:
        state_rows = running.astype(jnp.bfloat16).reshape(width, HD)
        msg_in = shift_up(jnp.concatenate([state_rows, tag_rows], axis=0), 1, n_seq)
        state_in = msg_in[:width].reshape(head_count, HD, HD).astype(jnp.float32)
        tag_in = msg_in[width, 0].astype(jnp.int32)
        joins = (my_index >= 1) & (tag_in == first_doc)
        if stage < reach:
            running = local_state + jnp.where(joins & whole_block, state_in, 0.0)
        else:
            carried = jnp.where(joins, state_in, jnp.zeros_like(state_in))

    split = head_count // 2
    query_msg = jnp.concatenate([soft_query, doc_cols], axis=1)
    query_msgs = [query_msg]
    for d in dists:
        if d == 2:
            query_msg = jnp.concatenate([query_msg[:, split * HD : width], query_msg[:, width:]], axis=1)
        query_msg = shift_down(query_msg, 1, n_seq)
        query_msgs.append(query_msg)
    far_width = (head_count - split) * HD
    next_queries = query_msgs[1][:, :width].reshape(row_count, head_count, HD)
    next_docs = query_msgs[1][:, width].astype(jnp.int32)
    far_queries = [next_queries[:, split:]] + [
        m[:, :far_width].reshape(row_count, head_count - split, HD) for m in query_msgs[2:]
    ]
    far_docs = [next_docs] + [m[:, far_width].astype(jnp.int32) for m in query_msgs[2:]]

    near_key = jnp.concatenate([soft_key[:, : split * HD], doc_cols], axis=1)
    key_msgs = [near_key]
    for d in dists[:-1]:
        key_msgs.append(shift_up(key_msgs[-1], 1, n_seq))
    key_blocks = [m[:, : split * HD].reshape(row_count, split, HD) for m in key_msgs]
    key_docs = [m[:, split * HD].astype(jnp.int32) for m in key_msgs]

    positions = jnp.arange(row_count, dtype=jnp.int32)
    causal = positions[:, None] >= positions[None, :]
    keep_local = causal & (doc_id[:, None] == doc_id[None, :])
    score_scale = 1.0 / math.sqrt(HD)
    key_soft = soft_key.reshape(row_count, head_count, HD)

    def weights_of(query_rows, key_all, keep):
        logits = (
            jnp.einsum("qhd,khd->hqk", query_rows, key_all, preferred_element_type=jnp.float32)
            * score_scale
        )
        logits = jnp.where(keep[None], logits, -1e30)
        row_max = jnp.max(logits, axis=-1)
        probs = jnp.where(keep[None], jnp.exp(logits - row_max[..., None]), 0.0)
        return probs.astype(jnp.bfloat16), row_max, jnp.sum(probs, axis=-1)

    diag = weights_of(soft_query.reshape(row_count, head_count, HD), key_soft, keep_local)
    valid = jnp.concatenate(
        [jnp.full((row_count,), my_index >= d, jnp.bool_) for d in range(len(key_blocks))]
    )
    keep_next = (next_docs[:, None] == jnp.concatenate(key_docs)[None, :]) & valid[None, :]
    near = weights_of(next_queries[:, :split], jnp.concatenate(key_blocks, axis=0), keep_next)
    far = [
        weights_of(far_queries[i], key_soft[:, split:], far_docs[i][:, None] == doc_id[None, :])
        for i in range(reach)
    ]

    scores = jnp.einsum("qhd,khd->hqk", queries, key_rows, preferred_element_type=jnp.float32)
    rounded = jnp.where(keep_local[None], scores, jnp.zeros_like(scores)).astype(jnp.bfloat16)
    block_term = jnp.einsum("hqk,khd->qhd", rounded, value_rows, preferred_element_type=jnp.float32)
    carried_term = jnp.einsum(
        "qhd,hde->qhe", queries.astype(jnp.float32), carried, precision=lax.Precision.HIGHEST
    )
    carried_term = jnp.where(
        (doc_id == first_doc)[:, None, None], carried_term, jnp.zeros_like(carried_term)
    )
    lin_raw = block_term + carried_term
    mean_square = jnp.mean(lin_raw * lin_raw, axis=-1, keepdims=True)
    gain_rows = norm_gain.astype(jnp.float32).reshape(head_count, HD)
    gate_rows = jax.nn.sigmoid(out_gate.astype(jnp.float32).reshape(row_count, head_count, HD))
    normed = lin_raw * lax.rsqrt(mean_square + norm_eps) * gain_rows * gate_rows
    lin_out = normed.astype(jnp.bfloat16).reshape(row_count, width)

    value_own = lin_out.reshape(row_count, head_count, HD)
    has_source = my_index >= 1

    def received(msg, stats):
        max_in = jnp.where(has_source, stats[0], -1e30)
        sum_in = jnp.where(has_source, stats[1], 0.0)
        return jnp.where(has_source, msg.astype(jnp.float32), 0.0), max_in, sum_in

    def mix(weights, value_block):
        return jnp.einsum("hqk,khd->qhd", weights, value_block, preferred_element_type=jnp.float32)

    near_values = [value_own[:, :split]]
    far_running = None
    for s in dists:
        d = reach + 1 - s
        far_probs, far_max, far_sum = far[d - 1]
        far_part = (mix(far_probs, value_own[:, split:]), far_max, far_sum)
        if far_running is not None:
            far_part = merge(far_running, far_part)
        if s < reach:
            near_msg = near_values[-1]
        else:
            probs, near_max, near_sum = near
            near_out = jnp.zeros((row_count, split, HD), jnp.float32)
            for k, value_block in enumerate(near_values):
                near_out = near_out + mix(
                    probs[:, :, k * row_count : (k + 1) * row_count], value_block
                )
            near_msg = near_out
            far_part = (
                jnp.concatenate([near_out, far_part[0]], axis=1),
                jnp.concatenate([near_max, far_part[1]], axis=0),
                jnp.concatenate([near_sum, far_part[2]], axis=0),
            )
        if s < reach:
            msg = jnp.concatenate([near_msg.astype(jnp.bfloat16), far_part[0].astype(jnp.bfloat16)], axis=1)
        else:
            msg = far_part[0].astype(jnp.bfloat16)
        msg_in = shift_up(msg, 1, n_seq)
        stats_in = shift_up(jnp.stack([far_part[1], far_part[2]]), 1, n_seq)
        if s < reach:
            near_values.append(msg_in[:, :split])
            far_running = received(msg_in[:, split:], stats_in)
        else:
            running_in = received(msg_in, stats_in)

    diag_probs, diag_max, diag_sum = diag
    diag_out = mix(diag_probs, value_own)
    mixed, row_max, row_sum = merge(running_in, (diag_out, diag_max, diag_sum))
    soft_out = mixed / jnp.transpose(row_sum)[:, :, None]
    return (lin_out, soft_out.astype(jnp.bfloat16).reshape(row_count, width))


def solution(mesh):
    return jax.shard_map(
        per_device,
        mesh=mesh,
        in_specs=(
            P(("grp", "seq"), "head"),
            P(("grp", "seq"), "head"),
            P(("grp", "seq"), "head"),
            P("head"),
            P(("grp", "seq"), "head"),
            P(("grp", "seq"), "head"),
            P(("grp", "seq"), "head"),
            P(("grp", "seq")),
        ),
        out_specs=(P(("grp", "seq"), "head"), P(("grp", "seq"), "head")),
        check_vma=False,
    )
```

```python
import math

import jax
import jax.numpy as jnp
from jax import lax
from jax.sharding import PartitionSpec as P

HD = 128


norm_eps = 1e-06


def shift_up(x, dist, n_seq):
    return lax.ppermute(x, "seq", [(s, s + dist) for s in range(n_seq - dist)])


def shift_down(x, dist, n_seq):
    return lax.ppermute(x, "seq", [(s + dist, s) for s in range(n_seq - dist)])


def merge(part_a, part_b):
    out_a, max_a, sum_a = part_a
    out_b, max_b, sum_b = part_b
    top = jnp.maximum(max_a, max_b)
    scale_a = jnp.exp(max_a - top)
    scale_b = jnp.exp(max_b - top)
    out = out_a * jnp.transpose(scale_a)[:, :, None] + out_b * jnp.transpose(scale_b)[:, :, None]
    return out, top, sum_a * scale_a + sum_b * scale_b


def general_softmax(soft_query, soft_key, doc_id, doc_cols, lin_out, diag, reach, n_seq, my_index):
    row_count, width = soft_query.shape
    head_count = width // HD
    dists = list(range(1, reach + 1))
    score_scale = 1.0 / math.sqrt(HD)

    def weights_of(query_rows, keep):
        logits = (
            jnp.einsum("qhd,khd->hqk", query_rows, key_all, preferred_element_type=jnp.float32)
            * score_scale
        )
        logits = jnp.where(keep[None], logits, -1e30)
        row_max = jnp.max(logits, axis=-1)
        probs = jnp.where(keep[None], jnp.exp(logits - row_max[..., None]), 0.0)
        return probs.astype(jnp.bfloat16), row_max, jnp.sum(probs, axis=-1)

    next_msg = shift_down(jnp.concatenate([soft_query, doc_cols], axis=1), 1, n_seq)
    next_queries = next_msg[:, :width].reshape(row_count, head_count, HD)
    next_docs = next_msg[:, width].astype(jnp.int32)
    key_msgs = [jnp.concatenate([soft_key, doc_cols], axis=1)]
    for d in dists[:-1]:
        key_msgs.append(shift_up(key_msgs[-1], 1, n_seq))
    key_blocks = [m[:, :width].reshape(row_count, head_count, HD) for m in key_msgs]
    key_docs = [m[:, width].astype(jnp.int32) for m in key_msgs]

    key_all = jnp.concatenate(key_blocks, axis=0)
    valid = jnp.concatenate(
        [jnp.full((row_count,), my_index >= d, jnp.bool_) for d in range(len(key_blocks))]
    )
    keep_next = (next_docs[:, None] == jnp.concatenate(key_docs)[None, :]) & valid[None, :]
    ahead = weights_of(next_queries, keep_next)

    value_blocks = [lin_out.reshape(row_count, head_count, HD)]
    for d in dists[:-1]:
        value_blocks.append(shift_up(value_blocks[-1], 1, n_seq))

    probs, ahead_max, ahead_sum = ahead
    ahead_out = jnp.zeros((row_count, head_count, HD), jnp.float32)
    for d, value_block in enumerate(value_blocks):
        ahead_out = ahead_out + jnp.einsum(
            "hqk,khd->qhd",
            probs[:, :, d * row_count : (d + 1) * row_count],
            value_block,
            preferred_element_type=jnp.float32,
        )
    out_in = shift_up(ahead_out.astype(jnp.bfloat16), 1, n_seq)
    stats_in = shift_up(jnp.stack([ahead_max, ahead_sum]), 1, n_seq)
    has_source = my_index >= 1
    max_in = jnp.where(has_source, stats_in[0], -1e30)
    sum_in = jnp.where(has_source, stats_in[1], 0.0)
    out_in = jnp.where(has_source, out_in.astype(jnp.float32), 0.0)

    diag_probs, diag_max, diag_sum = diag
    diag_out = jnp.einsum(
        "hqk,khd->qhd", diag_probs, value_blocks[0], preferred_element_type=jnp.float32
    )
    mixed, row_max, row_sum = merge((out_in, max_in, sum_in), (diag_out, diag_max, diag_sum))
    return mixed, row_max, row_sum


def per_device(lin_query, lin_key, lin_value, norm_gain, out_gate, soft_query, soft_key, doc_id):
    row_count = lin_query.shape[0]
    head_count = lin_query.shape[1] // HD
    n_seq = lax.axis_size("seq")
    my_index = lax.axis_index("seq")
    max_doc = n_seq * row_count // 2
    reach = min(n_seq - 1, (max_doc + row_count - 2) // row_count)
    dists = list(range(1, reach + 1))
    width = head_count * HD

    queries = lin_query.reshape(row_count, head_count, HD)
    key_rows = lin_key.reshape(row_count, head_count, HD)
    value_rows = lin_value.reshape(row_count, head_count, HD)
    first_doc = doc_id[0]
    last_doc = doc_id[-1]

    doc_cols = jnp.broadcast_to(doc_id.astype(jnp.bfloat16)[:, None], (row_count, HD))

    tail_keys = jnp.where((doc_id == last_doc)[:, None, None], key_rows, jnp.zeros_like(key_rows))
    local_state = jnp.einsum(
        "thd,the->hde", tail_keys, value_rows, preferred_element_type=jnp.float32
    )
    tag_rows = jnp.full((8, HD), last_doc, jnp.int32).astype(jnp.bfloat16)
    whole_block = first_doc == last_doc
    running = local_state
    for stage in dists:
        state_rows = running.astype(jnp.bfloat16).reshape(width, HD)
        msg_in = shift_up(jnp.concatenate([state_rows, tag_rows], axis=0), 1, n_seq)
        state_in = msg_in[:width].reshape(head_count, HD, HD).astype(jnp.float32)
        tag_in = msg_in[width, 0].astype(jnp.int32)
        joins = (my_index >= 1) & (tag_in == first_doc)
        if stage < reach:
            running = local_state + jnp.where(joins & whole_block, state_in, 0.0)
        else:
            carried = jnp.where(joins, state_in, jnp.zeros_like(state_in))

    positions = jnp.arange(row_count, dtype=jnp.int32)
    causal = positions[:, None] >= positions[None, :]
    keep_local = causal & (doc_id[:, None] == doc_id[None, :])
    score_scale = 1.0 / math.sqrt(HD)

    scores = jnp.einsum("qhd,khd->hqk", queries, key_rows, preferred_element_type=jnp.float32)
    rounded = jnp.where(keep_local[None], scores, jnp.zeros_like(scores)).astype(jnp.bfloat16)
    block_term = jnp.einsum("hqk,khd->qhd", rounded, value_rows, preferred_element_type=jnp.float32)
    carried_term = jnp.einsum(
        "qhd,hde->qhe", queries.astype(jnp.float32), carried, precision=lax.Precision.HIGHEST
    )
    carried_term = jnp.where(
        (doc_id == first_doc)[:, None, None], carried_term, jnp.zeros_like(carried_term)
    )
    lin_raw = block_term + carried_term
    mean_square = jnp.mean(lin_raw * lin_raw, axis=-1, keepdims=True)
    gain_rows = norm_gain.astype(jnp.float32).reshape(head_count, HD)
    gate_rows = jax.nn.sigmoid(out_gate.astype(jnp.float32).reshape(row_count, head_count, HD))
    normed = lin_raw * lax.rsqrt(mean_square + norm_eps) * gain_rows * gate_rows
    lin_out = normed.astype(jnp.bfloat16).reshape(row_count, width)

    def weights_of(query_rows, key_all, keep):
        logits = (
            jnp.einsum("qhd,khd->hqk", query_rows, key_all, preferred_element_type=jnp.float32)
            * score_scale
        )
        logits = jnp.where(keep[None], logits, -1e30)
        row_max = jnp.max(logits, axis=-1)
        probs = jnp.where(keep[None], jnp.exp(logits - row_max[..., None]), 0.0)
        return probs.astype(jnp.bfloat16), row_max, jnp.sum(probs, axis=-1)

    def mix(weights, value_block):
        return jnp.einsum("hqk,khd->qhd", weights, value_block, preferred_element_type=jnp.float32)

    has_source = my_index >= 1
    query_soft = soft_query.reshape(row_count, head_count, HD)
    key_soft = soft_key.reshape(row_count, head_count, HD)
    value_own = lin_out.reshape(row_count, head_count, HD)
    diag = weights_of(query_soft, key_soft, keep_local)
    window = (max_doc - row_count + 1) // 2
    if reach == 2 and n_seq >= 3 and 0 < window < row_count:
        cut = row_count - window
        query_msg = shift_down(jnp.concatenate([soft_query, doc_cols], axis=1), 1, n_seq)
        next_queries = query_msg[:, :width].reshape(row_count, head_count, HD)
        next_docs = query_msg[:, width].astype(jnp.int32)
        far_msg = shift_down(query_msg[:window], 1, n_seq)
        far_queries = far_msg[:, :width].reshape(window, head_count, HD)
        far_docs = far_msg[:, width].astype(jnp.int32)
        key_msg = shift_up(jnp.concatenate([soft_key, doc_cols], axis=1)[cut:], 1, n_seq)
        tail_keys_soft = key_msg[:, :width].reshape(window, head_count, HD)
        tail_docs = key_msg[:, width].astype(jnp.int32)
        below_tail = has_source & (tail_docs[0] != tail_docs[-1])
        own_tail = doc_id[cut] != doc_id[-1]

        far_probs, far_max, far_sum = weights_of(
            far_queries, key_soft, far_docs[:, None] == doc_id[None, :]
        )
        far_out = mix(far_probs, value_own)
        stage_msg = jnp.where(own_tail, value_own[cut:], far_out.astype(jnp.bfloat16))
        stage_in = shift_up(stage_msg, 1, n_seq)
        stats_in = shift_up(jnp.stack([far_max, far_sum]), 1, n_seq)

        keep_next = jnp.concatenate(
            [
                next_docs[:, None] == doc_id[None, :],
                (next_docs[:, None] == tail_docs[None, :]) & below_tail,
            ],
            axis=1,
        )
        probs, next_max, next_sum = weights_of(
            next_queries, jnp.concatenate([key_soft, tail_keys_soft], axis=0), keep_next
        )
        tail_values = jnp.where(below_tail, stage_in, jnp.zeros_like(stage_in))
        next_out = mix(probs[:, :, :row_count], value_own) + mix(probs[:, :, row_count:], tail_values)
        use_far = has_source & jnp.logical_not(below_tail)
        pad = row_count - window
        far_in = (
            jnp.concatenate(
                [jnp.where(use_far, stage_in.astype(jnp.float32), 0.0),
                 jnp.zeros((pad, head_count, HD), jnp.float32)], axis=0
            ),
            jnp.concatenate(
                [jnp.where(use_far, stats_in[0], -1e30),
                 jnp.full((head_count, pad), -1e30, jnp.float32)], axis=1
            ),
            jnp.concatenate(
                [jnp.where(use_far, stats_in[1], 0.0),
                 jnp.zeros((head_count, pad), jnp.float32)], axis=1
            ),
        )
        next_out, next_max, next_sum = merge(far_in, (next_out, next_max, next_sum))
        out_in = shift_up(next_out.astype(jnp.bfloat16), 1, n_seq)
        stats_in = shift_up(jnp.stack([next_max, next_sum]), 1, n_seq)
        running_in = (
            jnp.where(has_source, out_in.astype(jnp.float32), 0.0),
            jnp.where(has_source, stats_in[0], -1e30),
            jnp.where(has_source, stats_in[1], 0.0),
        )
        diag_probs, diag_max, diag_sum = diag
        mixed, row_max, row_sum = merge(running_in, (mix(diag_probs, value_own), diag_max, diag_sum))
    else:
        mixed, row_max, row_sum = general_softmax(
            soft_query, soft_key, doc_id, doc_cols, lin_out, diag, reach, n_seq, my_index
        )
    soft_out = mixed / jnp.transpose(row_sum)[:, :, None]
    return (lin_out, soft_out.astype(jnp.bfloat16).reshape(row_count, width))


def solution(mesh):
    return jax.shard_map(
        per_device,
        mesh=mesh,
        in_specs=(
            P(("grp", "seq"), "head"),
            P(("grp", "seq"), "head"),
            P(("grp", "seq"), "head"),
            P("head"),
            P(("grp", "seq"), "head"),
            P(("grp", "seq"), "head"),
            P(("grp", "seq"), "head"),
            P(("grp", "seq")),
        ),
        out_specs=(P(("grp", "seq"), "head"), P(("grp", "seq"), "head")),
        check_vma=False,
    )
```

```python
import math

import jax
import jax.numpy as jnp
from jax import lax
from jax.sharding import PartitionSpec as P

HD = 128


norm_eps = 1e-06


def shift_up(x, dist, n_seq):
    return lax.ppermute(x, "seq", [(s, s + dist) for s in range(n_seq - dist)])


def shift_down(x, dist, n_seq):
    return lax.ppermute(x, "seq", [(s + dist, s) for s in range(n_seq - dist)])


def merge(part_a, part_b):
    out_a, max_a, sum_a = part_a
    out_b, max_b, sum_b = part_b
    top = jnp.maximum(max_a, max_b)
    scale_a = jnp.exp(max_a - top)
    scale_b = jnp.exp(max_b - top)
    out = out_a * jnp.transpose(scale_a)[:, :, None] + out_b * jnp.transpose(scale_b)[:, :, None]
    return out, top, sum_a * scale_a + sum_b * scale_b


def general_softmax(soft_query, soft_key, doc_id, doc_cols, lin_out, diag, reach, n_seq, my_index):
    row_count, width = soft_query.shape
    head_count = width // HD
    dists = list(range(1, reach + 1))
    score_scale = 1.0 / math.sqrt(HD)

    def weights_of(query_rows, keep):
        logits = (
            jnp.einsum("qhd,khd->hqk", query_rows, key_all, preferred_element_type=jnp.float32)
            * score_scale
        )
        logits = jnp.where(keep[None], logits, -1e30)
        row_max = jnp.max(logits, axis=-1)
        probs = jnp.where(keep[None], jnp.exp(logits - row_max[..., None]), 0.0)
        return probs.astype(jnp.bfloat16), row_max, jnp.sum(probs, axis=-1)

    next_msg = shift_down(jnp.concatenate([soft_query, doc_cols], axis=1), 1, n_seq)
    next_queries = next_msg[:, :width].reshape(row_count, head_count, HD)
    next_docs = next_msg[:, width].astype(jnp.int32)
    key_msgs = [jnp.concatenate([soft_key, doc_cols], axis=1)]
    for d in dists[:-1]:
        key_msgs.append(shift_up(key_msgs[-1], 1, n_seq))
    key_blocks = [m[:, :width].reshape(row_count, head_count, HD) for m in key_msgs]
    key_docs = [m[:, width].astype(jnp.int32) for m in key_msgs]

    key_all = jnp.concatenate(key_blocks, axis=0)
    valid = jnp.concatenate(
        [jnp.full((row_count,), my_index >= d, jnp.bool_) for d in range(len(key_blocks))]
    )
    keep_next = (next_docs[:, None] == jnp.concatenate(key_docs)[None, :]) & valid[None, :]
    ahead = weights_of(next_queries, keep_next)

    value_blocks = [lin_out.reshape(row_count, head_count, HD)]
    for d in dists[:-1]:
        value_blocks.append(shift_up(value_blocks[-1], 1, n_seq))

    probs, ahead_max, ahead_sum = ahead
    ahead_out = jnp.zeros((row_count, head_count, HD), jnp.float32)
    for d, value_block in enumerate(value_blocks):
        ahead_out = ahead_out + jnp.einsum(
            "hqk,khd->qhd",
            probs[:, :, d * row_count : (d + 1) * row_count],
            value_block,
            preferred_element_type=jnp.float32,
        )
    out_in = shift_up(ahead_out.astype(jnp.bfloat16), 1, n_seq)
    stats_in = shift_up(jnp.stack([ahead_max, ahead_sum]), 1, n_seq)
    has_source = my_index >= 1
    max_in = jnp.where(has_source, stats_in[0], -1e30)
    sum_in = jnp.where(has_source, stats_in[1], 0.0)
    out_in = jnp.where(has_source, out_in.astype(jnp.float32), 0.0)

    diag_probs, diag_max, diag_sum = diag
    diag_out = jnp.einsum(
        "hqk,khd->qhd", diag_probs, value_blocks[0], preferred_element_type=jnp.float32
    )
    mixed, row_max, row_sum = merge((out_in, max_in, sum_in), (diag_out, diag_max, diag_sum))
    return mixed, row_max, row_sum


def per_device(lin_query, lin_key, lin_value, norm_gain, out_gate, soft_query, soft_key, doc_id):
    row_count = lin_query.shape[0]
    head_count = lin_query.shape[1] // HD
    n_seq = lax.axis_size("seq")
    my_index = lax.axis_index("seq")
    max_doc = n_seq * row_count // 2
    reach = min(n_seq - 1, (max_doc + row_count - 2) // row_count)
    dists = list(range(1, reach + 1))
    width = head_count * HD

    queries = lin_query.reshape(row_count, head_count, HD)
    key_rows = lin_key.reshape(row_count, head_count, HD)
    value_rows = lin_value.reshape(row_count, head_count, HD)
    first_doc = doc_id[0]
    last_doc = doc_id[-1]

    doc_cols = jnp.broadcast_to(doc_id.astype(jnp.bfloat16)[:, None], (row_count, HD))

    tail_keys = jnp.where((doc_id == last_doc)[:, None, None], key_rows, jnp.zeros_like(key_rows))
    local_state = jnp.einsum(
        "thd,the->hde", tail_keys, value_rows, preferred_element_type=jnp.float32
    )
    tag_rows = jnp.full((8, HD), last_doc, jnp.int32).astype(jnp.bfloat16)
    whole_block = first_doc == last_doc
    running = local_state
    for stage in dists:
        state_rows = running.astype(jnp.bfloat16).reshape(width, HD)
        msg_in = shift_up(jnp.concatenate([state_rows, tag_rows], axis=0), 1, n_seq)
        state_in = msg_in[:width].reshape(head_count, HD, HD).astype(jnp.float32)
        tag_in = msg_in[width, 0].astype(jnp.int32)
        joins = (my_index >= 1) & (tag_in == first_doc)
        if stage < reach:
            running = local_state + jnp.where(joins & whole_block, state_in, 0.0)
        else:
            carried = jnp.where(joins, state_in, jnp.zeros_like(state_in))

    positions = jnp.arange(row_count, dtype=jnp.int32)
    causal = positions[:, None] >= positions[None, :]
    keep_local = causal & (doc_id[:, None] == doc_id[None, :])
    score_scale = 1.0 / math.sqrt(HD)

    def weights_of(query_rows, key_all, keep):
        logits = (
            jnp.einsum("qhd,khd->hqk", query_rows, key_all, preferred_element_type=jnp.float32)
            * score_scale
        )
        logits = jnp.where(keep[None], logits, -1e30)
        row_max = jnp.max(logits, axis=-1)
        probs = jnp.where(keep[None], jnp.exp(logits - row_max[..., None]), 0.0)
        return probs.astype(jnp.bfloat16), row_max, jnp.sum(probs, axis=-1)

    query_soft = soft_query.reshape(row_count, head_count, HD)
    key_soft = soft_key.reshape(row_count, head_count, HD)
    diag = weights_of(query_soft, key_soft, keep_local)
    if reach == 2:
        carried, diag = lax.optimization_barrier((carried, diag))

    scores = jnp.einsum("qhd,khd->hqk", queries, key_rows, preferred_element_type=jnp.float32)
    rounded = jnp.where(keep_local[None], scores, jnp.zeros_like(scores)).astype(jnp.bfloat16)
    block_term = jnp.einsum("hqk,khd->qhd", rounded, value_rows, preferred_element_type=jnp.float32)
    carried_term = jnp.einsum(
        "qhd,hde->qhe", queries.astype(jnp.float32), carried, precision=lax.Precision.HIGHEST
    )
    carried_term = jnp.where(
        (doc_id == first_doc)[:, None, None], carried_term, jnp.zeros_like(carried_term)
    )
    lin_raw = block_term + carried_term
    mean_square = jnp.mean(lin_raw * lin_raw, axis=-1, keepdims=True)
    gain_rows = norm_gain.astype(jnp.float32).reshape(head_count, HD)
    gate_rows = jax.nn.sigmoid(out_gate.astype(jnp.float32).reshape(row_count, head_count, HD))
    normed = lin_raw * lax.rsqrt(mean_square + norm_eps) * gain_rows * gate_rows
    lin_out = normed.astype(jnp.bfloat16).reshape(row_count, width)

    def mix(weights, value_block):
        return jnp.einsum("hqk,khd->qhd", weights, value_block, preferred_element_type=jnp.float32)

    has_source = my_index >= 1
    value_own = lin_out.reshape(row_count, head_count, HD)
    window = (max_doc - row_count + 1) // 2
    if reach == 2 and n_seq >= 3 and 0 < window < row_count:
        cut = row_count - window
        query_msg = shift_down(jnp.concatenate([soft_query, doc_cols], axis=1), 1, n_seq)
        next_queries = query_msg[:, :width].reshape(row_count, head_count, HD)
        next_docs = query_msg[:, width].astype(jnp.int32)
        far_msg = shift_down(query_msg[:window], 1, n_seq)
        lin_out, query_msg = lax.optimization_barrier((lin_out, query_msg))
        value_own = lin_out.reshape(row_count, head_count, HD)
        next_queries = query_msg[:, :width].reshape(row_count, head_count, HD)
        next_docs = query_msg[:, width].astype(jnp.int32)
        far_queries = far_msg[:, :width].reshape(window, head_count, HD)
        far_docs = far_msg[:, width].astype(jnp.int32)
        key_msg = shift_up(jnp.concatenate([soft_key, doc_cols], axis=1)[cut:], 1, n_seq)
        tail_keys_soft = key_msg[:, :width].reshape(window, head_count, HD)
        tail_docs = key_msg[:, width].astype(jnp.int32)
        below_tail = has_source & (tail_docs[0] != tail_docs[-1])
        own_tail = doc_id[cut] != doc_id[-1]

        far_probs, far_max, far_sum = weights_of(
            far_queries, key_soft, far_docs[:, None] == doc_id[None, :]
        )
        far_out = mix(far_probs, value_own)
        stage_msg = jnp.where(own_tail, value_own[cut:], far_out.astype(jnp.bfloat16))
        stage_in = shift_up(stage_msg, 1, n_seq)
        stats_in = shift_up(jnp.stack([far_max, far_sum]), 1, n_seq)

        keep_next = jnp.concatenate(
            [
                next_docs[:, None] == doc_id[None, :],
                (next_docs[:, None] == tail_docs[None, :]) & below_tail,
            ],
            axis=1,
        )
        probs, next_max, next_sum = weights_of(
            next_queries, jnp.concatenate([key_soft, tail_keys_soft], axis=0), keep_next
        )
        tail_values = jnp.where(below_tail, stage_in, jnp.zeros_like(stage_in))
        next_out = mix(probs[:, :, :row_count], value_own) + mix(probs[:, :, row_count:], tail_values)
        use_far = has_source & jnp.logical_not(below_tail)
        pad = row_count - window
        far_in = (
            jnp.concatenate(
                [jnp.where(use_far, stage_in.astype(jnp.float32), 0.0),
                 jnp.zeros((pad, head_count, HD), jnp.float32)], axis=0
            ),
            jnp.concatenate(
                [jnp.where(use_far, stats_in[0], -1e30),
                 jnp.full((head_count, pad), -1e30, jnp.float32)], axis=1
            ),
            jnp.concatenate(
                [jnp.where(use_far, stats_in[1], 0.0),
                 jnp.zeros((head_count, pad), jnp.float32)], axis=1
            ),
        )
        next_out, next_max, next_sum = merge(far_in, (next_out, next_max, next_sum))
        out_in = shift_up(next_out.astype(jnp.bfloat16), 1, n_seq)
        stats_in = shift_up(jnp.stack([next_max, next_sum]), 1, n_seq)
        running_in = (
            jnp.where(has_source, out_in.astype(jnp.float32), 0.0),
            jnp.where(has_source, stats_in[0], -1e30),
            jnp.where(has_source, stats_in[1], 0.0),
        )
        diag_probs, diag_max, diag_sum = diag
        mixed, row_max, row_sum = merge(running_in, (mix(diag_probs, value_own), diag_max, diag_sum))
    else:
        mixed, row_max, row_sum = general_softmax(
            soft_query, soft_key, doc_id, doc_cols, lin_out, diag, reach, n_seq, my_index
        )
    soft_out = mixed / jnp.transpose(row_sum)[:, :, None]
    return (lin_out, soft_out.astype(jnp.bfloat16).reshape(row_count, width))


def solution(mesh):
    return jax.shard_map(
        per_device,
        mesh=mesh,
        in_specs=(
            P(("grp", "seq"), "head"),
            P(("grp", "seq"), "head"),
            P(("grp", "seq"), "head"),
            P("head"),
            P(("grp", "seq"), "head"),
            P(("grp", "seq"), "head"),
            P(("grp", "seq"), "head"),
            P(("grp", "seq")),
        ),
        out_specs=(P(("grp", "seq"), "head"), P(("grp", "seq"), "head")),
        check_vma=False,
    )
```

```python
import math

import jax
import jax.numpy as jnp
from jax import lax
from jax.sharding import PartitionSpec as P

HD = 128


norm_eps = 1e-06


def shift_up(x, dist, n_seq):
    return lax.ppermute(x, "seq", [(s, s + dist) for s in range(n_seq - dist)])


def shift_down(x, dist, n_seq):
    return lax.ppermute(x, "seq", [(s + dist, s) for s in range(n_seq - dist)])


def merge(part_a, part_b):
    out_a, max_a, sum_a = part_a
    out_b, max_b, sum_b = part_b
    top = jnp.maximum(max_a, max_b)
    scale_a = jnp.exp(max_a - top)
    scale_b = jnp.exp(max_b - top)
    out = out_a * jnp.transpose(scale_a)[:, :, None] + out_b * jnp.transpose(scale_b)[:, :, None]
    return out, top, sum_a * scale_a + sum_b * scale_b


def general_softmax(soft_query, soft_key, doc_id, doc_cols, lin_out, diag, reach, n_seq, my_index):
    row_count, width = soft_query.shape
    head_count = width // HD
    dists = list(range(1, reach + 1))
    score_scale = 1.0 / math.sqrt(HD)

    def weights_of(query_rows, keep):
        logits = (
            jnp.einsum("qhd,khd->hqk", query_rows, key_all, preferred_element_type=jnp.float32)
            * score_scale
        )
        logits = jnp.where(keep[None], logits, -1e30)
        row_max = jnp.max(logits, axis=-1)
        probs = jnp.where(keep[None], jnp.exp(logits - row_max[..., None]), 0.0)
        return probs.astype(jnp.bfloat16), row_max, jnp.sum(probs, axis=-1)

    next_msg = shift_down(jnp.concatenate([soft_query, doc_cols], axis=1), 1, n_seq)
    next_queries = next_msg[:, :width].reshape(row_count, head_count, HD)
    next_docs = next_msg[:, width].astype(jnp.int32)
    key_msgs = [jnp.concatenate([soft_key, doc_cols], axis=1)]
    for d in dists[:-1]:
        key_msgs.append(shift_up(key_msgs[-1], 1, n_seq))
    key_blocks = [m[:, :width].reshape(row_count, head_count, HD) for m in key_msgs]
    key_docs = [m[:, width].astype(jnp.int32) for m in key_msgs]

    key_all = jnp.concatenate(key_blocks, axis=0)
    valid = jnp.concatenate(
        [jnp.full((row_count,), my_index >= d, jnp.bool_) for d in range(len(key_blocks))]
    )
    keep_next = (next_docs[:, None] == jnp.concatenate(key_docs)[None, :]) & valid[None, :]
    ahead = weights_of(next_queries, keep_next)

    value_blocks = [lin_out.reshape(row_count, head_count, HD)]
    for d in dists[:-1]:
        value_blocks.append(shift_up(value_blocks[-1], 1, n_seq))

    probs, ahead_max, ahead_sum = ahead
    ahead_out = jnp.zeros((row_count, head_count, HD), jnp.float32)
    for d, value_block in enumerate(value_blocks):
        ahead_out = ahead_out + jnp.einsum(
            "hqk,khd->qhd",
            probs[:, :, d * row_count : (d + 1) * row_count],
            value_block,
            preferred_element_type=jnp.float32,
        )
    out_in = shift_up(ahead_out.astype(jnp.bfloat16), 1, n_seq)
    stats_in = shift_up(jnp.stack([ahead_max, ahead_sum]), 1, n_seq)
    has_source = my_index >= 1
    max_in = jnp.where(has_source, stats_in[0], -1e30)
    sum_in = jnp.where(has_source, stats_in[1], 0.0)
    out_in = jnp.where(has_source, out_in.astype(jnp.float32), 0.0)

    diag_probs, diag_max, diag_sum = diag
    diag_out = jnp.einsum(
        "hqk,khd->qhd", diag_probs, value_blocks[0], preferred_element_type=jnp.float32
    )
    mixed, row_max, row_sum = merge((out_in, max_in, sum_in), (diag_out, diag_max, diag_sum))
    return mixed, row_max, row_sum


def per_device(lin_query, lin_key, lin_value, norm_gain, out_gate, soft_query, soft_key, doc_id):
    row_count = lin_query.shape[0]
    head_count = lin_query.shape[1] // HD
    n_seq = lax.axis_size("seq")
    my_index = lax.axis_index("seq")
    max_doc = n_seq * row_count // 2
    reach = min(n_seq - 1, (max_doc + row_count - 2) // row_count)
    dists = list(range(1, reach + 1))
    width = head_count * HD

    queries = lin_query.reshape(row_count, head_count, HD)
    key_rows = lin_key.reshape(row_count, head_count, HD)
    value_rows = lin_value.reshape(row_count, head_count, HD)
    first_doc = doc_id[0]
    last_doc = doc_id[-1]

    doc_cols = jnp.broadcast_to(doc_id.astype(jnp.bfloat16)[:, None], (row_count, HD))

    tail_keys = jnp.where((doc_id == last_doc)[:, None, None], key_rows, jnp.zeros_like(key_rows))
    local_state = jnp.einsum(
        "thd,the->hde", tail_keys, value_rows, preferred_element_type=jnp.float32
    )
    tag_rows = jnp.full((8, HD), last_doc, jnp.int32).astype(jnp.bfloat16)
    whole_block = first_doc == last_doc
    running = local_state
    for stage in dists:
        state_rows = running.astype(jnp.bfloat16).reshape(width, HD)
        msg_in = shift_up(jnp.concatenate([state_rows, tag_rows], axis=0), 1, n_seq)
        state_in = msg_in[:width].reshape(head_count, HD, HD).astype(jnp.float32)
        tag_in = msg_in[width, 0].astype(jnp.int32)
        joins = (my_index >= 1) & (tag_in == first_doc)
        if stage < reach:
            running = local_state + jnp.where(joins & whole_block, state_in, 0.0)
        else:
            carried = jnp.where(joins, state_in, jnp.zeros_like(state_in))

    positions = jnp.arange(row_count, dtype=jnp.int32)
    causal = positions[:, None] >= positions[None, :]
    keep_local = causal & (doc_id[:, None] == doc_id[None, :])
    score_scale = 1.0 / math.sqrt(HD)

    def weights_of(query_rows, key_all, keep):
        logits = (
            jnp.einsum("qhd,khd->hqk", query_rows, key_all, preferred_element_type=jnp.float32)
            * score_scale
        )
        logits = jnp.where(keep[None], logits, -1e30)
        row_max = jnp.max(logits, axis=-1)
        probs = jnp.where(keep[None], jnp.exp(logits - row_max[..., None]), 0.0)
        return probs.astype(jnp.bfloat16), row_max, jnp.sum(probs, axis=-1)

    query_soft = soft_query.reshape(row_count, head_count, HD)
    key_soft = soft_key.reshape(row_count, head_count, HD)
    diag = weights_of(query_soft, key_soft, keep_local)
    if reach == 2:
        carried, diag = lax.optimization_barrier((carried, diag))

    scores = jnp.einsum("qhd,khd->hqk", queries, key_rows, preferred_element_type=jnp.float32)
    rounded = jnp.where(keep_local[None], scores, jnp.zeros_like(scores)).astype(jnp.bfloat16)
    block_term = jnp.einsum("hqk,khd->qhd", rounded, value_rows, preferred_element_type=jnp.float32)
    carried_term = jnp.einsum(
        "qhd,hde->qhe", queries.astype(jnp.float32), carried, precision=lax.Precision.HIGHEST
    )
    carried_term = jnp.where(
        (doc_id == first_doc)[:, None, None], carried_term, jnp.zeros_like(carried_term)
    )
    lin_raw = block_term + carried_term
    mean_square = jnp.mean(lin_raw * lin_raw, axis=-1, keepdims=True)
    gain_rows = norm_gain.astype(jnp.float32).reshape(head_count, HD)
    gate_rows = jax.nn.sigmoid(out_gate.astype(jnp.float32).reshape(row_count, head_count, HD))
    normed = lin_raw * lax.rsqrt(mean_square + norm_eps) * gain_rows * gate_rows
    lin_out = normed.astype(jnp.bfloat16).reshape(row_count, width)

    def mix(weights, value_block):
        return jnp.einsum("hqk,khd->qhd", weights, value_block, preferred_element_type=jnp.float32)

    has_source = my_index >= 1
    value_own = lin_out.reshape(row_count, head_count, HD)
    window = (max_doc - row_count + 1) // 2
    if reach == 2 and n_seq >= 3 and 0 < window < row_count:
        cut = row_count - window
        query_msg = shift_down(jnp.concatenate([soft_query, doc_cols], axis=1), 1, n_seq)
        next_queries = query_msg[:, :width].reshape(row_count, head_count, HD)
        next_docs = query_msg[:, width].astype(jnp.int32)
        far_msg = shift_down(query_msg[:window], 1, n_seq)
        far_queries = far_msg[:, :width].reshape(window, head_count, HD)
        far_docs = far_msg[:, width].astype(jnp.int32)
        key_msg = shift_up(jnp.concatenate([soft_key, doc_cols], axis=1)[cut:], 1, n_seq)
        tail_keys_soft = key_msg[:, :width].reshape(window, head_count, HD)
        tail_docs = key_msg[:, width].astype(jnp.int32)
        below_tail = has_source & (tail_docs[0] != tail_docs[-1])
        own_tail = doc_id[cut] != doc_id[-1]

        far_probs, far_max, far_sum = weights_of(
            far_queries, key_soft, far_docs[:, None] == doc_id[None, :]
        )
        far_out = mix(far_probs, value_own)
        stage_msg = jnp.where(own_tail, value_own[cut:], far_out.astype(jnp.bfloat16))
        stage_in = shift_up(stage_msg, 1, n_seq)
        stats_in = shift_up(jnp.stack([far_max, far_sum]), 1, n_seq)

        keep_next = jnp.concatenate(
            [
                next_docs[:, None] == doc_id[None, :],
                (next_docs[:, None] == tail_docs[None, :]) & below_tail,
            ],
            axis=1,
        )
        probs, next_max, next_sum = weights_of(
            next_queries, jnp.concatenate([key_soft, tail_keys_soft], axis=0), keep_next
        )
        tail_values = jnp.where(below_tail, stage_in, jnp.zeros_like(stage_in))
        next_out = mix(probs[:, :, :row_count], value_own) + mix(probs[:, :, row_count:], tail_values)
        use_far = has_source & jnp.logical_not(below_tail)
        pad = row_count - window
        far_in = (
            jnp.concatenate(
                [jnp.where(use_far, stage_in.astype(jnp.float32), 0.0),
                 jnp.zeros((pad, head_count, HD), jnp.float32)], axis=0
            ),
            jnp.concatenate(
                [jnp.where(use_far, stats_in[0], -1e30),
                 jnp.full((head_count, pad), -1e30, jnp.float32)], axis=1
            ),
            jnp.concatenate(
                [jnp.where(use_far, stats_in[1], 0.0),
                 jnp.zeros((head_count, pad), jnp.float32)], axis=1
            ),
        )
        next_out, next_max, next_sum = merge(far_in, (next_out, next_max, next_sum))
        out_in = shift_up(next_out.astype(jnp.bfloat16), 1, n_seq)
        stats_in = shift_up(jnp.stack([next_max, next_sum]), 1, n_seq)
        running_in = (
            jnp.where(has_source, out_in.astype(jnp.float32), 0.0),
            jnp.where(has_source, stats_in[0], -1e30),
            jnp.where(has_source, stats_in[1], 0.0),
        )
        diag_probs, diag_max, diag_sum = diag
        mixed, row_max, row_sum = merge(running_in, (mix(diag_probs, value_own), diag_max, diag_sum))
    else:
        mixed, row_max, row_sum = general_softmax(
            soft_query, soft_key, doc_id, doc_cols, lin_out, diag, reach, n_seq, my_index
        )
    soft_out = mixed / jnp.transpose(row_sum)[:, :, None]
    return (lin_out, soft_out.astype(jnp.bfloat16).reshape(row_count, width))


def solution(mesh):
    return jax.shard_map(
        per_device,
        mesh=mesh,
        in_specs=(
            P(("grp", "seq"), "head"),
            P(("grp", "seq"), "head"),
            P(("grp", "seq"), "head"),
            P("head"),
            P(("grp", "seq"), "head"),
            P(("grp", "seq"), "head"),
            P(("grp", "seq"), "head"),
            P(("grp", "seq")),
        ),
        out_specs=(P(("grp", "seq"), "head"), P(("grp", "seq"), "head")),
        check_vma=False,
    )
```

```python
import math

import jax
import jax.numpy as jnp
from jax import lax
from jax.sharding import PartitionSpec as P

HD = 128


norm_eps = 1e-06


def shift_up(x, dist, n_seq):
    return lax.ppermute(x, "seq", [(s, s + dist) for s in range(n_seq - dist)])


def shift_down(x, dist, n_seq):
    return lax.ppermute(x, "seq", [(s + dist, s) for s in range(n_seq - dist)])


def merge(part_a, part_b):
    out_a, max_a, sum_a = part_a
    out_b, max_b, sum_b = part_b
    top = jnp.maximum(max_a, max_b)
    scale_a = jnp.exp(max_a - top)
    scale_b = jnp.exp(max_b - top)
    out = out_a * jnp.transpose(scale_a)[:, :, None] + out_b * jnp.transpose(scale_b)[:, :, None]
    return out, top, sum_a * scale_a + sum_b * scale_b


def per_device(lin_query, lin_key, lin_value, norm_gain, out_gate, soft_query, soft_key, doc_id):
    row_count = lin_query.shape[0]
    head_count = lin_query.shape[1] // HD
    n_seq = lax.axis_size("seq")
    my_index = lax.axis_index("seq")
    max_doc = n_seq * row_count // 2
    reach = min(n_seq - 1, (max_doc + row_count - 2) // row_count)
    dists = list(range(1, reach + 1))
    width = head_count * HD

    queries = lin_query.reshape(row_count, head_count, HD)
    key_rows = lin_key.reshape(row_count, head_count, HD)
    value_rows = lin_value.reshape(row_count, head_count, HD)
    first_doc = doc_id[0]
    last_doc = doc_id[-1]

    doc_cols = jnp.broadcast_to(doc_id.astype(jnp.bfloat16)[:, None], (row_count, HD))

    tail_keys = jnp.where((doc_id == last_doc)[:, None, None], key_rows, jnp.zeros_like(key_rows))
    local_state = jnp.einsum(
        "thd,the->hde", tail_keys, value_rows, preferred_element_type=jnp.float32
    )
    tag_rows = jnp.full((8, HD), last_doc, jnp.int32).astype(jnp.bfloat16)
    whole_block = first_doc == last_doc
    running = local_state
    for stage in dists:
        state_rows = running.astype(jnp.bfloat16).reshape(width, HD)
        msg_in = shift_up(jnp.concatenate([state_rows, tag_rows], axis=0), 1, n_seq)
        state_in = msg_in[:width].reshape(head_count, HD, HD).astype(jnp.float32)
        tag_in = msg_in[width, 0].astype(jnp.int32)
        joins = (my_index >= 1) & (tag_in == first_doc)
        if stage < reach:
            running = local_state + jnp.where(joins & whole_block, state_in, 0.0)
        else:
            carried = jnp.where(joins, state_in, jnp.zeros_like(state_in))

    next_msg = shift_down(jnp.concatenate([soft_query, doc_cols], axis=1), 1, n_seq)
    next_queries = next_msg[:, :width].reshape(row_count, head_count, HD)
    next_docs = next_msg[:, width].astype(jnp.int32)
    key_msgs = [jnp.concatenate([soft_key, doc_cols], axis=1)]
    for d in dists[:-1]:
        key_msgs.append(shift_up(key_msgs[-1], 1, n_seq))
    key_blocks = [m[:, :width].reshape(row_count, head_count, HD) for m in key_msgs]
    key_docs = [m[:, width].astype(jnp.int32) for m in key_msgs]

    positions = jnp.arange(row_count, dtype=jnp.int32)
    causal = positions[:, None] >= positions[None, :]
    keep_local = causal & (doc_id[:, None] == doc_id[None, :])
    score_scale = 1.0 / math.sqrt(HD)

    def weights_of(query_rows, keep):
        logits = (
            jnp.einsum("qhd,khd->hqk", query_rows, key_all, preferred_element_type=jnp.float32)
            * score_scale
        )
        logits = jnp.where(keep[None], logits, -1e30)
        row_max = jnp.max(logits, axis=-1)
        probs = jnp.where(keep[None], jnp.exp(logits - row_max[..., None]), 0.0)
        return probs.astype(jnp.bfloat16), row_max, jnp.sum(probs, axis=-1)

    key_all = key_blocks[0]
    diag = weights_of(soft_query.reshape(row_count, head_count, HD), keep_local)
    key_all = jnp.concatenate(key_blocks, axis=0)
    valid = jnp.concatenate(
        [jnp.full((row_count,), my_index >= d, jnp.bool_) for d in range(len(key_blocks))]
    )
    keep_next = (next_docs[:, None] == jnp.concatenate(key_docs)[None, :]) & valid[None, :]
    ahead = weights_of(next_queries, keep_next)

    scores = jnp.einsum("qhd,khd->hqk", queries, key_rows, preferred_element_type=jnp.float32)
    rounded = jnp.where(keep_local[None], scores, jnp.zeros_like(scores)).astype(jnp.bfloat16)
    block_term = jnp.einsum("hqk,khd->qhd", rounded, value_rows, preferred_element_type=jnp.float32)
    carried_term = jnp.einsum(
        "qhd,hde->qhe", queries.astype(jnp.float32), carried, precision=lax.Precision.HIGHEST
    )
    carried_term = jnp.where(
        (doc_id == first_doc)[:, None, None], carried_term, jnp.zeros_like(carried_term)
    )
    lin_raw = block_term + carried_term
    mean_square = jnp.mean(lin_raw * lin_raw, axis=-1, keepdims=True)
    gain_rows = norm_gain.astype(jnp.float32).reshape(head_count, HD)
    gate_rows = jax.nn.sigmoid(out_gate.astype(jnp.float32).reshape(row_count, head_count, HD))
    normed = lin_raw * lax.rsqrt(mean_square + norm_eps) * gain_rows * gate_rows
    lin_out = normed.astype(jnp.bfloat16).reshape(row_count, width)

    value_own = lin_out.reshape(row_count, head_count, HD)
    probs, ahead_max, ahead_sum = ahead
    diag_probs, diag_max, diag_sum = diag
    has_source = my_index >= 1
    half = head_count // 2
    pieces = []
    for lo, hi in ((0, half), (half, head_count)):
        value_blocks = [value_own[:, lo:hi]]
        for d in dists[:-1]:
            value_blocks.append(shift_up(value_blocks[-1], 1, n_seq))
        ahead_out = jnp.zeros((row_count, hi - lo, HD), jnp.float32)
        for d, value_block in enumerate(value_blocks):
            ahead_out = ahead_out + jnp.einsum(
                "hqk,khd->qhd",
                probs[lo:hi, :, d * row_count : (d + 1) * row_count],
                value_block,
                preferred_element_type=jnp.float32,
            )
        out_in = shift_up(ahead_out.astype(jnp.bfloat16), 1, n_seq)
        stats_in = shift_up(jnp.stack([ahead_max[lo:hi], ahead_sum[lo:hi]]), 1, n_seq)
        max_in = jnp.where(has_source, stats_in[0], -1e30)
        sum_in = jnp.where(has_source, stats_in[1], 0.0)
        out_in = jnp.where(has_source, out_in.astype(jnp.float32), 0.0)
        diag_out = jnp.einsum(
            "hqk,khd->qhd", diag_probs[lo:hi], value_blocks[0], preferred_element_type=jnp.float32
        )
        mixed, row_max, row_sum = merge(
            (out_in, max_in, sum_in), (diag_out, diag_max[lo:hi], diag_sum[lo:hi])
        )
        pieces.append(mixed / jnp.transpose(row_sum)[:, :, None])
    soft_out = jnp.concatenate(pieces, axis=1)
    return (lin_out, soft_out.astype(jnp.bfloat16).reshape(row_count, width))


def solution(mesh):
    return jax.shard_map(
        per_device,
        mesh=mesh,
        in_specs=(
            P(("grp", "seq"), "head"),
            P(("grp", "seq"), "head"),
            P(("grp", "seq"), "head"),
            P("head"),
            P(("grp", "seq"), "head"),
            P(("grp", "seq"), "head"),
            P(("grp", "seq"), "head"),
            P(("grp", "seq")),
        ),
        out_specs=(P(("grp", "seq"), "head"), P(("grp", "seq"), "head")),
        check_vma=False,
    )
```

```python
import math

import jax
import jax.numpy as jnp
from jax import lax
from jax.sharding import PartitionSpec as P

HD = 128


norm_eps = 1e-06


def shift_up(x, dist, n_seq):
    return lax.ppermute(x, "seq", [(s, s + dist) for s in range(n_seq - dist)])


def shift_down(x, dist, n_seq):
    return lax.ppermute(x, "seq", [(s + dist, s) for s in range(n_seq - dist)])


def merge(part_a, part_b):
    out_a, max_a, sum_a = part_a
    out_b, max_b, sum_b = part_b
    top = jnp.maximum(max_a, max_b)
    scale_a = jnp.exp(max_a - top)
    scale_b = jnp.exp(max_b - top)
    out = out_a * jnp.transpose(scale_a)[:, :, None] + out_b * jnp.transpose(scale_b)[:, :, None]
    return out, top, sum_a * scale_a + sum_b * scale_b


def per_device(lin_query, lin_key, lin_value, norm_gain, out_gate, soft_query, soft_key, doc_id):
    row_count = lin_query.shape[0]
    head_count = lin_query.shape[1] // HD
    n_seq = lax.axis_size("seq")
    my_index = lax.axis_index("seq")
    max_doc = n_seq * row_count // 2
    reach = min(n_seq - 1, (max_doc + row_count - 2) // row_count)
    dists = list(range(1, reach + 1))
    width = head_count * HD

    queries = lin_query.reshape(row_count, head_count, HD)
    key_rows = lin_key.reshape(row_count, head_count, HD)
    value_rows = lin_value.reshape(row_count, head_count, HD)
    first_doc = doc_id[0]
    last_doc = doc_id[-1]

    doc_cols = jnp.broadcast_to(doc_id.astype(jnp.bfloat16)[:, None], (row_count, HD))

    tail_keys = jnp.where((doc_id == last_doc)[:, None, None], key_rows, jnp.zeros_like(key_rows))
    local_state = jnp.einsum(
        "thd,the->hde", tail_keys, value_rows, preferred_element_type=jnp.float32
    )
    tag_rows = jnp.full((8, HD), last_doc, jnp.int32).astype(jnp.bfloat16)
    whole_block = first_doc == last_doc
    running = local_state
    for stage in dists:
        state_rows = running.astype(jnp.bfloat16).reshape(width, HD)
        msg_in = shift_up(jnp.concatenate([state_rows, tag_rows], axis=0), 1, n_seq)
        state_in = msg_in[:width].reshape(head_count, HD, HD).astype(jnp.float32)
        tag_in = msg_in[width, 0].astype(jnp.int32)
        joins = (my_index >= 1) & (tag_in == first_doc)
        if stage < reach:
            running = local_state + jnp.where(joins & whole_block, state_in, 0.0)
        else:
            carried = jnp.where(joins, state_in, jnp.zeros_like(state_in))

    next_msg = shift_down(jnp.concatenate([soft_query, doc_cols], axis=1), 1, n_seq)
    next_queries = next_msg[:, :width].reshape(row_count, head_count, HD)
    next_docs = next_msg[:, width].astype(jnp.int32)
    key_msgs = [jnp.concatenate([soft_key, doc_cols], axis=1)]
    for d in dists[:-1]:
        key_msgs.append(shift_up(key_msgs[-1], 1, n_seq))
    key_blocks = [m[:, :width].reshape(row_count, head_count, HD) for m in key_msgs]
    key_docs = [m[:, width].astype(jnp.int32) for m in key_msgs]

    positions = jnp.arange(row_count, dtype=jnp.int32)
    causal = positions[:, None] >= positions[None, :]
    keep_local = causal & (doc_id[:, None] == doc_id[None, :])
    score_scale = 1.0 / math.sqrt(HD)

    def weights_of(query_rows, keep):
        logits = (
            jnp.einsum("qhd,khd->hqk", query_rows, key_all, preferred_element_type=jnp.float32)
            * score_scale
        )
        logits = jnp.where(keep[None], logits, -1e30)
        row_max = jnp.max(logits, axis=-1)
        probs = jnp.where(keep[None], jnp.exp(logits - row_max[..., None]), 0.0)
        return probs.astype(jnp.bfloat16), row_max, jnp.sum(probs, axis=-1)

    key_all = key_blocks[0]
    diag = weights_of(soft_query.reshape(row_count, head_count, HD), keep_local)
    key_all = jnp.concatenate(key_blocks, axis=0)
    valid = jnp.concatenate(
        [jnp.full((row_count,), my_index >= d, jnp.bool_) for d in range(len(key_blocks))]
    )
    keep_next = (next_docs[:, None] == jnp.concatenate(key_docs)[None, :]) & valid[None, :]
    ahead = weights_of(next_queries, keep_next)

    scores = jnp.einsum("qhd,khd->hqk", queries, key_rows, preferred_element_type=jnp.float32)
    rounded = jnp.where(keep_local[None], scores, jnp.zeros_like(scores)).astype(jnp.bfloat16)
    block_term = jnp.einsum("hqk,khd->qhd", rounded, value_rows, preferred_element_type=jnp.float32)
    carried_term = jnp.einsum(
        "qhd,hde->qhe", queries.astype(jnp.float32), carried, precision=lax.Precision.HIGHEST
    )
    carried_term = jnp.where(
        (doc_id == first_doc)[:, None, None], carried_term, jnp.zeros_like(carried_term)
    )
    lin_raw = block_term + carried_term
    mean_square = jnp.mean(lin_raw * lin_raw, axis=-1, keepdims=True)
    gain_rows = norm_gain.astype(jnp.float32).reshape(head_count, HD)
    gate_rows = jax.nn.sigmoid(out_gate.astype(jnp.float32).reshape(row_count, head_count, HD))
    normed = lin_raw * lax.rsqrt(mean_square + norm_eps) * gain_rows * gate_rows
    lin_out = normed.astype(jnp.bfloat16).reshape(row_count, width)

    value_own = lin_out.reshape(row_count, head_count, HD)
    probs, ahead_max, ahead_sum = ahead
    diag_probs, diag_max, diag_sum = diag
    has_source = my_index >= 1
    group = head_count // 4 if head_count % 4 == 0 else head_count // 2
    pieces = []
    for lo in range(0, head_count, group):
        hi = min(lo + group, head_count)
        value_blocks = [value_own[:, lo:hi]]
        for d in dists[:-1]:
            value_blocks.append(shift_up(value_blocks[-1], 1, n_seq))
        ahead_out = jnp.zeros((row_count, hi - lo, HD), jnp.float32)
        for d, value_block in enumerate(value_blocks):
            ahead_out = ahead_out + jnp.einsum(
                "hqk,khd->qhd",
                probs[lo:hi, :, d * row_count : (d + 1) * row_count],
                value_block,
                preferred_element_type=jnp.float32,
            )
        out_in = shift_up(ahead_out.astype(jnp.bfloat16), 1, n_seq)
        stats_in = shift_up(jnp.stack([ahead_max[lo:hi], ahead_sum[lo:hi]]), 1, n_seq)
        max_in = jnp.where(has_source, stats_in[0], -1e30)
        sum_in = jnp.where(has_source, stats_in[1], 0.0)
        out_in = jnp.where(has_source, out_in.astype(jnp.float32), 0.0)
        diag_out = jnp.einsum(
            "hqk,khd->qhd", diag_probs[lo:hi], value_blocks[0], preferred_element_type=jnp.float32
        )
        mixed, row_max, row_sum = merge(
            (out_in, max_in, sum_in), (diag_out, diag_max[lo:hi], diag_sum[lo:hi])
        )
        pieces.append(mixed / jnp.transpose(row_sum)[:, :, None])
    soft_out = jnp.concatenate(pieces, axis=1)
    return (lin_out, soft_out.astype(jnp.bfloat16).reshape(row_count, width))


def solution(mesh):
    return jax.shard_map(
        per_device,
        mesh=mesh,
        in_specs=(
            P(("grp", "seq"), "head"),
            P(("grp", "seq"), "head"),
            P(("grp", "seq"), "head"),
            P("head"),
            P(("grp", "seq"), "head"),
            P(("grp", "seq"), "head"),
            P(("grp", "seq"), "head"),
            P(("grp", "seq")),
        ),
        out_specs=(P(("grp", "seq"), "head"), P(("grp", "seq"), "head")),
        check_vma=False,
    )
```

```python
import math

import jax
import jax.numpy as jnp
from jax import lax
from jax.sharding import PartitionSpec as P

HD = 128


norm_eps = 1e-06


def shift_up(x, dist, n_seq):
    return lax.ppermute(x, "seq", [(s, s + dist) for s in range(n_seq - dist)])


def shift_down(x, dist, n_seq):
    return lax.ppermute(x, "seq", [(s + dist, s) for s in range(n_seq - dist)])


def merge(part_a, part_b):
    out_a, max_a, sum_a = part_a
    out_b, max_b, sum_b = part_b
    top = jnp.maximum(max_a, max_b)
    scale_a = jnp.exp(max_a - top)
    scale_b = jnp.exp(max_b - top)
    out = out_a * jnp.transpose(scale_a)[:, :, None] + out_b * jnp.transpose(scale_b)[:, :, None]
    return out, top, sum_a * scale_a + sum_b * scale_b


def per_device(lin_query, lin_key, lin_value, norm_gain, out_gate, soft_query, soft_key, doc_id):
    row_count = lin_query.shape[0]
    head_count = lin_query.shape[1] // HD
    n_seq = lax.axis_size("seq")
    my_index = lax.axis_index("seq")
    max_doc = n_seq * row_count // 2
    reach = min(n_seq - 1, (max_doc + row_count - 2) // row_count)
    dists = list(range(1, reach + 1))
    width = head_count * HD

    queries = lin_query.reshape(row_count, head_count, HD)
    key_rows = lin_key.reshape(row_count, head_count, HD)
    value_rows = lin_value.reshape(row_count, head_count, HD)
    first_doc = doc_id[0]
    last_doc = doc_id[-1]

    doc_cols = jnp.broadcast_to(doc_id.astype(jnp.bfloat16)[:, None], (row_count, HD))

    tail_keys = jnp.where((doc_id == last_doc)[:, None, None], key_rows, jnp.zeros_like(key_rows))
    local_state = jnp.einsum(
        "thd,the->hde", tail_keys, value_rows, preferred_element_type=jnp.float32
    )
    tag_rows = jnp.full((8, HD), last_doc, jnp.int32).astype(jnp.bfloat16)
    whole_block = first_doc == last_doc
    running = local_state
    for stage in dists:
        state_rows = running.astype(jnp.bfloat16).reshape(width, HD)
        msg_in = shift_up(jnp.concatenate([state_rows, tag_rows], axis=0), 1, n_seq)
        state_in = msg_in[:width].reshape(head_count, HD, HD).astype(jnp.float32)
        tag_in = msg_in[width, 0].astype(jnp.int32)
        joins = (my_index >= 1) & (tag_in == first_doc)
        if stage < reach:
            running = local_state + jnp.where(joins & whole_block, state_in, 0.0)
        else:
            carried = jnp.where(joins, state_in, jnp.zeros_like(state_in))

    next_msg = shift_down(jnp.concatenate([soft_query, doc_cols], axis=1), 1, n_seq)
    next_queries = next_msg[:, :width].reshape(row_count, head_count, HD)
    next_docs = next_msg[:, width].astype(jnp.int32)
    key_msgs = [jnp.concatenate([soft_key, doc_cols], axis=1)]
    for d in dists[:-1]:
        key_msgs.append(shift_up(key_msgs[-1], 1, n_seq))
    key_blocks = [m[:, :width].reshape(row_count, head_count, HD) for m in key_msgs]
    key_docs = [m[:, width].astype(jnp.int32) for m in key_msgs]

    positions = jnp.arange(row_count, dtype=jnp.int32)
    causal = positions[:, None] >= positions[None, :]
    keep_local = causal & (doc_id[:, None] == doc_id[None, :])
    score_scale = 1.0 / math.sqrt(HD)

    def weights_of(query_rows, keep):
        logits = (
            jnp.einsum("qhd,khd->hqk", query_rows, key_all, preferred_element_type=jnp.float32)
            * score_scale
        )
        logits = jnp.where(keep[None], logits, -1e30)
        row_max = jnp.max(logits, axis=-1)
        probs = jnp.where(keep[None], jnp.exp(logits - row_max[..., None]), 0.0)
        return probs.astype(jnp.bfloat16), row_max, jnp.sum(probs, axis=-1)

    key_all = key_blocks[0]
    diag = weights_of(soft_query.reshape(row_count, head_count, HD), keep_local)
    key_all = jnp.concatenate(key_blocks, axis=0)
    valid = jnp.concatenate(
        [jnp.full((row_count,), my_index >= d, jnp.bool_) for d in range(len(key_blocks))]
    )
    keep_next = (next_docs[:, None] == jnp.concatenate(key_docs)[None, :]) & valid[None, :]
    ahead = weights_of(next_queries, keep_next)

    def lightning(lo, hi):
        q, k, v = queries[:, lo:hi], key_rows[:, lo:hi], value_rows[:, lo:hi]
        scores = jnp.einsum("qhd,khd->hqk", q, k, preferred_element_type=jnp.float32)
        rounded = jnp.where(keep_local[None], scores, jnp.zeros_like(scores)).astype(jnp.bfloat16)
        block_term = jnp.einsum("hqk,khd->qhd", rounded, v, preferred_element_type=jnp.float32)
        carried_term = jnp.einsum(
            "qhd,hde->qhe", q.astype(jnp.float32), carried[lo:hi], precision=lax.Precision.HIGHEST
        )
        carried_term = jnp.where(
            (doc_id == first_doc)[:, None, None], carried_term, jnp.zeros_like(carried_term)
        )
        lin_raw = block_term + carried_term
        mean_square = jnp.mean(lin_raw * lin_raw, axis=-1, keepdims=True)
        gain_rows = norm_gain.astype(jnp.float32).reshape(head_count, HD)[lo:hi]
        gate_rows = jax.nn.sigmoid(
            out_gate.astype(jnp.float32).reshape(row_count, head_count, HD)[:, lo:hi]
        )
        normed = lin_raw * lax.rsqrt(mean_square + norm_eps) * gain_rows * gate_rows
        return normed.astype(jnp.bfloat16)

    probs, ahead_max, ahead_sum = ahead
    diag_probs, diag_max, diag_sum = diag
    has_source = my_index >= 1
    half = head_count // 2
    pieces = []
    lin_pieces = []
    for lo, hi in ((0, half), (half, head_count)):
        value_half = lightning(lo, hi)
        lin_pieces.append(value_half)
        value_blocks = [value_half]
        for d in dists[:-1]:
            value_blocks.append(shift_up(value_blocks[-1], 1, n_seq))
        ahead_out = jnp.zeros((row_count, hi - lo, HD), jnp.float32)
        for d, value_block in enumerate(value_blocks):
            ahead_out = ahead_out + jnp.einsum(
                "hqk,khd->qhd",
                probs[lo:hi, :, d * row_count : (d + 1) * row_count],
                value_block,
                preferred_element_type=jnp.float32,
            )
        out_in = shift_up(ahead_out.astype(jnp.bfloat16), 1, n_seq)
        stats_in = shift_up(jnp.stack([ahead_max[lo:hi], ahead_sum[lo:hi]]), 1, n_seq)
        max_in = jnp.where(has_source, stats_in[0], -1e30)
        sum_in = jnp.where(has_source, stats_in[1], 0.0)
        out_in = jnp.where(has_source, out_in.astype(jnp.float32), 0.0)
        diag_out = jnp.einsum(
            "hqk,khd->qhd", diag_probs[lo:hi], value_blocks[0], preferred_element_type=jnp.float32
        )
        mixed, row_max, row_sum = merge(
            (out_in, max_in, sum_in), (diag_out, diag_max[lo:hi], diag_sum[lo:hi])
        )
        pieces.append(mixed / jnp.transpose(row_sum)[:, :, None])
    soft_out = jnp.concatenate(pieces, axis=1)
    lin_out = jnp.concatenate(lin_pieces, axis=1).reshape(row_count, width)
    return (lin_out, soft_out.astype(jnp.bfloat16).reshape(row_count, width))


def solution(mesh):
    return jax.shard_map(
        per_device,
        mesh=mesh,
        in_specs=(
            P(("grp", "seq"), "head"),
            P(("grp", "seq"), "head"),
            P(("grp", "seq"), "head"),
            P("head"),
            P(("grp", "seq"), "head"),
            P(("grp", "seq"), "head"),
            P(("grp", "seq"), "head"),
            P(("grp", "seq")),
        ),
        out_specs=(P(("grp", "seq"), "head"), P(("grp", "seq"), "head")),
        check_vma=False,
    )
```

```python
import math

import jax
import jax.numpy as jnp
from jax import lax
from jax.sharding import PartitionSpec as P

HD = 128


norm_eps = 1e-06


def shift_up(x, dist, n_seq):
    return lax.ppermute(x, "seq", [(s, s + dist) for s in range(n_seq - dist)])


def shift_down(x, dist, n_seq):
    return lax.ppermute(x, "seq", [(s + dist, s) for s in range(n_seq - dist)])


def merge(part_a, part_b):
    out_a, max_a, sum_a = part_a
    out_b, max_b, sum_b = part_b
    top = jnp.maximum(max_a, max_b)
    scale_a = jnp.exp(max_a - top)
    scale_b = jnp.exp(max_b - top)
    out = out_a * jnp.transpose(scale_a)[:, :, None] + out_b * jnp.transpose(scale_b)[:, :, None]
    return out, top, sum_a * scale_a + sum_b * scale_b


def per_device(lin_query, lin_key, lin_value, norm_gain, out_gate, soft_query, soft_key, doc_id):
    row_count = lin_query.shape[0]
    head_count = lin_query.shape[1] // HD
    n_seq = lax.axis_size("seq")
    my_index = lax.axis_index("seq")
    max_doc = n_seq * row_count // 2
    reach = min(n_seq - 1, (max_doc + row_count - 2) // row_count)
    dists = list(range(1, reach + 1))
    width = head_count * HD

    queries = lin_query.reshape(row_count, head_count, HD)
    key_rows = lin_key.reshape(row_count, head_count, HD)
    value_rows = lin_value.reshape(row_count, head_count, HD)
    first_doc = doc_id[0]
    last_doc = doc_id[-1]

    doc_cols = jnp.broadcast_to(doc_id.astype(jnp.bfloat16)[:, None], (row_count, HD))

    tail_keys = jnp.where((doc_id == last_doc)[:, None, None], key_rows, jnp.zeros_like(key_rows))
    local_state = jnp.einsum(
        "thd,the->hde", tail_keys, value_rows, preferred_element_type=jnp.float32
    )
    tag_rows = jnp.full((8, HD), last_doc, jnp.int32).astype(jnp.bfloat16)
    whole_block = first_doc == last_doc
    running = local_state
    for stage in dists:
        state_rows = running.astype(jnp.bfloat16).reshape(width, HD)
        msg_in = shift_up(jnp.concatenate([state_rows, tag_rows], axis=0), 1, n_seq)
        state_in = msg_in[:width].reshape(head_count, HD, HD).astype(jnp.float32)
        tag_in = msg_in[width, 0].astype(jnp.int32)
        joins = (my_index >= 1) & (tag_in == first_doc)
        if stage < reach:
            running = local_state + jnp.where(joins & whole_block, state_in, 0.0)
        else:
            carried = jnp.where(joins, state_in, jnp.zeros_like(state_in))

    next_msg = shift_down(jnp.concatenate([soft_query, doc_cols], axis=1), 1, n_seq)
    next_queries = next_msg[:, :width].reshape(row_count, head_count, HD)
    next_docs = next_msg[:, width].astype(jnp.int32)
    half = head_count // 2
    late_keys, _ = lax.optimization_barrier((soft_key[:, half * HD :], carried))
    key_msgs = [jnp.concatenate([soft_key[:, : half * HD], doc_cols], axis=1)]
    late_msgs = [late_keys]
    for d in dists[:-1]:
        key_msgs.append(shift_up(key_msgs[-1], 1, n_seq))
        late_msgs.append(shift_up(late_msgs[-1], 1, n_seq))
    key_halves = [
        [m[:, : half * HD].reshape(row_count, half, HD) for m in key_msgs],
        [m.reshape(row_count, head_count - half, HD) for m in late_msgs],
    ]
    key_docs = [m[:, half * HD].astype(jnp.int32) for m in key_msgs]

    positions = jnp.arange(row_count, dtype=jnp.int32)
    causal = positions[:, None] >= positions[None, :]
    keep_local = causal & (doc_id[:, None] == doc_id[None, :])
    score_scale = 1.0 / math.sqrt(HD)

    def weights_of(query_rows, keep):
        logits = (
            jnp.einsum("qhd,khd->hqk", query_rows, key_all, preferred_element_type=jnp.float32)
            * score_scale
        )
        logits = jnp.where(keep[None], logits, -1e30)
        row_max = jnp.max(logits, axis=-1)
        probs = jnp.where(keep[None], jnp.exp(logits - row_max[..., None]), 0.0)
        return probs.astype(jnp.bfloat16), row_max, jnp.sum(probs, axis=-1)

    key_all = soft_key.reshape(row_count, head_count, HD)
    diag = weights_of(soft_query.reshape(row_count, head_count, HD), keep_local)
    valid = jnp.concatenate(
        [jnp.full((row_count,), my_index >= d, jnp.bool_) for d in range(len(key_docs))]
    )
    keep_next = (next_docs[:, None] == jnp.concatenate(key_docs)[None, :]) & valid[None, :]
    aheads = []
    for (lo, hi), blocks in zip(((0, half), (half, head_count)), key_halves):
        key_all = jnp.concatenate(blocks, axis=0)
        aheads.append(weights_of(next_queries[:, lo:hi], keep_next))

    scores = jnp.einsum("qhd,khd->hqk", queries, key_rows, preferred_element_type=jnp.float32)
    rounded = jnp.where(keep_local[None], scores, jnp.zeros_like(scores)).astype(jnp.bfloat16)
    block_term = jnp.einsum("hqk,khd->qhd", rounded, value_rows, preferred_element_type=jnp.float32)
    carried_term = jnp.einsum(
        "qhd,hde->qhe", queries.astype(jnp.float32), carried, precision=lax.Precision.HIGHEST
    )
    carried_term = jnp.where(
        (doc_id == first_doc)[:, None, None], carried_term, jnp.zeros_like(carried_term)
    )
    lin_raw = block_term + carried_term
    mean_square = jnp.mean(lin_raw * lin_raw, axis=-1, keepdims=True)
    gain_rows = norm_gain.astype(jnp.float32).reshape(head_count, HD)
    gate_rows = jax.nn.sigmoid(out_gate.astype(jnp.float32).reshape(row_count, head_count, HD))
    normed = lin_raw * lax.rsqrt(mean_square + norm_eps) * gain_rows * gate_rows
    lin_out = normed.astype(jnp.bfloat16).reshape(row_count, width)

    value_own = lin_out.reshape(row_count, head_count, HD)
    diag_probs, diag_max, diag_sum = diag
    has_source = my_index >= 1
    pieces = []
    for (lo, hi), (probs, ahead_max, ahead_sum) in zip(((0, half), (half, head_count)), aheads):
        value_blocks = [value_own[:, lo:hi]]
        for d in dists[:-1]:
            value_blocks.append(shift_up(value_blocks[-1], 1, n_seq))
        ahead_out = jnp.zeros((row_count, hi - lo, HD), jnp.float32)
        for d, value_block in enumerate(value_blocks):
            ahead_out = ahead_out + jnp.einsum(
                "hqk,khd->qhd",
                probs[:, :, d * row_count : (d + 1) * row_count],
                value_block,
                preferred_element_type=jnp.float32,
            )
        out_in = shift_up(ahead_out.astype(jnp.bfloat16), 1, n_seq)
        stats_in = shift_up(jnp.stack([ahead_max, ahead_sum]), 1, n_seq)
        max_in = jnp.where(has_source, stats_in[0], -1e30)
        sum_in = jnp.where(has_source, stats_in[1], 0.0)
        out_in = jnp.where(has_source, out_in.astype(jnp.float32), 0.0)
        diag_out = jnp.einsum(
            "hqk,khd->qhd", diag_probs[lo:hi], value_blocks[0], preferred_element_type=jnp.float32
        )
        mixed, row_max, row_sum = merge(
            (out_in, max_in, sum_in), (diag_out, diag_max[lo:hi], diag_sum[lo:hi])
        )
        pieces.append(mixed / jnp.transpose(row_sum)[:, :, None])
    soft_out = jnp.concatenate(pieces, axis=1)
    return (lin_out, soft_out.astype(jnp.bfloat16).reshape(row_count, width))


def solution(mesh):
    return jax.shard_map(
        per_device,
        mesh=mesh,
        in_specs=(
            P(("grp", "seq"), "head"),
            P(("grp", "seq"), "head"),
            P(("grp", "seq"), "head"),
            P("head"),
            P(("grp", "seq"), "head"),
            P(("grp", "seq"), "head"),
            P(("grp", "seq"), "head"),
            P(("grp", "seq")),
        ),
        out_specs=(P(("grp", "seq"), "head"), P(("grp", "seq"), "head")),
        check_vma=False,
    )
```

```python
import math

import jax
import jax.numpy as jnp
from jax import lax
from jax.sharding import PartitionSpec as P

HD = 128


norm_eps = 1e-06


def shift_up(x, dist, n_seq):
    return lax.ppermute(x, "seq", [(s, s + dist) for s in range(n_seq - dist)])


def shift_down(x, dist, n_seq):
    return lax.ppermute(x, "seq", [(s + dist, s) for s in range(n_seq - dist)])


def merge(part_a, part_b):
    out_a, max_a, sum_a = part_a
    out_b, max_b, sum_b = part_b
    top = jnp.maximum(max_a, max_b)
    scale_a = jnp.exp(max_a - top)
    scale_b = jnp.exp(max_b - top)
    out = out_a * jnp.transpose(scale_a)[:, :, None] + out_b * jnp.transpose(scale_b)[:, :, None]
    return out, top, sum_a * scale_a + sum_b * scale_b


def per_device(lin_query, lin_key, lin_value, norm_gain, out_gate, soft_query, soft_key, doc_id):
    row_count = lin_query.shape[0]
    head_count = lin_query.shape[1] // HD
    n_seq = lax.axis_size("seq")
    my_index = lax.axis_index("seq")
    max_doc = n_seq * row_count // 2
    reach = min(n_seq - 1, (max_doc + row_count - 2) // row_count)
    dists = list(range(1, reach + 1))
    width = head_count * HD

    queries = lin_query.reshape(row_count, head_count, HD)
    key_rows = lin_key.reshape(row_count, head_count, HD)
    value_rows = lin_value.reshape(row_count, head_count, HD)
    first_doc = doc_id[0]
    last_doc = doc_id[-1]

    doc_cols = jnp.broadcast_to(doc_id.astype(jnp.bfloat16)[:, None], (row_count, HD))

    tail_keys = jnp.where((doc_id == last_doc)[:, None, None], key_rows, jnp.zeros_like(key_rows))
    local_state = jnp.einsum(
        "thd,the->hde", tail_keys, value_rows, preferred_element_type=jnp.float32
    )
    tag_rows = jnp.full((8, HD), last_doc, jnp.int32).astype(jnp.bfloat16)
    whole_block = first_doc == last_doc
    running = local_state
    for stage in dists:
        state_rows = running.astype(jnp.bfloat16).reshape(width, HD)
        msg_in = shift_up(jnp.concatenate([state_rows, tag_rows], axis=0), 1, n_seq)
        state_in = msg_in[:width].reshape(head_count, HD, HD).astype(jnp.float32)
        tag_in = msg_in[width, 0].astype(jnp.int32)
        joins = (my_index >= 1) & (tag_in == first_doc)
        if stage < reach:
            running = local_state + jnp.where(joins & whole_block, state_in, 0.0)
        else:
            carried = jnp.where(joins, state_in, jnp.zeros_like(state_in))

    next_msg = shift_down(jnp.concatenate([soft_query, doc_cols], axis=1), 1, n_seq)
    next_queries = next_msg[:, :width].reshape(row_count, head_count, HD)
    next_docs = next_msg[:, width].astype(jnp.int32)
    half = head_count // 2
    late_keys, _ = lax.optimization_barrier(
        (jnp.concatenate([soft_key[:, half * HD :], doc_cols], axis=1), carried)
    )
    key_msgs = [soft_key[:, : half * HD]]
    late_msgs = [late_keys]
    for d in dists[:-1]:
        key_msgs.append(shift_up(key_msgs[-1], 1, n_seq))
        late_msgs.append(shift_up(late_msgs[-1], 1, n_seq))
    key_halves = [
        [m.reshape(row_count, half, HD) for m in key_msgs],
        [m[:, : width - half * HD].reshape(row_count, head_count - half, HD) for m in late_msgs],
    ]
    key_docs = [m[:, width - half * HD].astype(jnp.int32) for m in late_msgs]

    positions = jnp.arange(row_count, dtype=jnp.int32)
    causal = positions[:, None] >= positions[None, :]
    keep_local = causal & (doc_id[:, None] == doc_id[None, :])
    score_scale = 1.0 / math.sqrt(HD)

    def weights_of(query_rows, keep):
        logits = (
            jnp.einsum("qhd,khd->hqk", query_rows, key_all, preferred_element_type=jnp.float32)
            * score_scale
        )
        logits = jnp.where(keep[None], logits, -1e30)
        row_max = jnp.max(logits, axis=-1)
        probs = jnp.where(keep[None], jnp.exp(logits - row_max[..., None]), 0.0)
        return probs.astype(jnp.bfloat16), row_max, jnp.sum(probs, axis=-1)

    key_all = soft_key.reshape(row_count, head_count, HD)
    diag = weights_of(soft_query.reshape(row_count, head_count, HD), keep_local)
    valid = jnp.concatenate(
        [jnp.full((row_count,), my_index >= d, jnp.bool_) for d in range(len(key_docs))]
    )
    keep_next = (next_docs[:, None] == jnp.concatenate(key_docs)[None, :]) & valid[None, :]
    aheads = []
    for (lo, hi), blocks in zip(((0, half), (half, head_count)), key_halves):
        key_all = jnp.concatenate(blocks, axis=0)
        aheads.append(weights_of(next_queries[:, lo:hi], keep_next))

    scores = jnp.einsum("qhd,khd->hqk", queries, key_rows, preferred_element_type=jnp.float32)
    rounded = jnp.where(keep_local[None], scores, jnp.zeros_like(scores)).astype(jnp.bfloat16)
    block_term = jnp.einsum("hqk,khd->qhd", rounded, value_rows, preferred_element_type=jnp.float32)
    carried_term = jnp.einsum(
        "qhd,hde->qhe", queries.astype(jnp.float32), carried, precision=lax.Precision.HIGHEST
    )
    carried_term = jnp.where(
        (doc_id == first_doc)[:, None, None], carried_term, jnp.zeros_like(carried_term)
    )
    lin_raw = block_term + carried_term
    mean_square = jnp.mean(lin_raw * lin_raw, axis=-1, keepdims=True)
    gain_rows = norm_gain.astype(jnp.float32).reshape(head_count, HD)
    gate_rows = jax.nn.sigmoid(out_gate.astype(jnp.float32).reshape(row_count, head_count, HD))
    normed = lin_raw * lax.rsqrt(mean_square + norm_eps) * gain_rows * gate_rows
    lin_out = normed.astype(jnp.bfloat16).reshape(row_count, width)

    value_own = lin_out.reshape(row_count, head_count, HD)
    diag_probs, diag_max, diag_sum = diag
    has_source = my_index >= 1
    pieces = []
    for (lo, hi), (probs, ahead_max, ahead_sum) in zip(((0, half), (half, head_count)), aheads):
        value_blocks = [value_own[:, lo:hi]]
        for d in dists[:-1]:
            value_blocks.append(shift_up(value_blocks[-1], 1, n_seq))
        ahead_out = jnp.zeros((row_count, hi - lo, HD), jnp.float32)
        for d, value_block in enumerate(value_blocks):
            ahead_out = ahead_out + jnp.einsum(
                "hqk,khd->qhd",
                probs[:, :, d * row_count : (d + 1) * row_count],
                value_block,
                preferred_element_type=jnp.float32,
            )
        out_in = shift_up(ahead_out.astype(jnp.bfloat16), 1, n_seq)
        stats_in = shift_up(jnp.stack([ahead_max, ahead_sum]), 1, n_seq)
        max_in = jnp.where(has_source, stats_in[0], -1e30)
        sum_in = jnp.where(has_source, stats_in[1], 0.0)
        out_in = jnp.where(has_source, out_in.astype(jnp.float32), 0.0)
        diag_out = jnp.einsum(
            "hqk,khd->qhd", diag_probs[lo:hi], value_blocks[0], preferred_element_type=jnp.float32
        )
        mixed, row_max, row_sum = merge(
            (out_in, max_in, sum_in), (diag_out, diag_max[lo:hi], diag_sum[lo:hi])
        )
        pieces.append(mixed / jnp.transpose(row_sum)[:, :, None])
    soft_out = jnp.concatenate(pieces, axis=1)
    return (lin_out, soft_out.astype(jnp.bfloat16).reshape(row_count, width))


def solution(mesh):
    return jax.shard_map(
        per_device,
        mesh=mesh,
        in_specs=(
            P(("grp", "seq"), "head"),
            P(("grp", "seq"), "head"),
            P(("grp", "seq"), "head"),
            P("head"),
            P(("grp", "seq"), "head"),
            P(("grp", "seq"), "head"),
            P(("grp", "seq"), "head"),
            P(("grp", "seq")),
        ),
        out_specs=(P(("grp", "seq"), "head"), P(("grp", "seq"), "head")),
        check_vma=False,
    )
```
